128 devices in a mesh: seq: 16 (over z, x_hi, core), head: 8 (over y, x_lo).
Axes of the slice: x: 4 (x_hi: 2, x_lo: 2; x = x_hi * 2 + x_lo), y: 4, z: 4, core: 2. Of those that a mesh axis runs over, the one named last changes fastest.
Arguments:
- queries: bfloat16 [16384, 4096], P('seq', 'head'), may hold values from -6 to 6
- key_rows: bfloat16 [16384, 4096], P('seq', 'head'), may hold values from -6 to 6
- value_rows: bfloat16 [16384, 4096], P('seq', 'head'), may hold values from -6 to 6
- out_weight: bfloat16 [4096, 4096], P('head'), may hold values from -0.375 to 0.375
- cotangent: bfloat16 [16384, 4096], P('seq', 'head'), may hold values from -1.5 to 1.5
- pattern: int32 [128, 7], P('seq'), may hold values 0 or 1
Outputs:
- output: bfloat16 [16384, 4096], P('seq', 'head')
- grad_query: bfloat16 [16384, 4096], P('seq', 'head')
- grad_keys: bfloat16 [16384, 4096], P('seq', 'head')
- grad_values: bfloat16 [16384, 4096], P('seq', 'head')
- grad_weight: float32 [4096, 4096], P('seq', 'head')
The draws below stay inside these ranges and needn't reach their ends.
All inputs are finite; a program needn't handle non-finite values. No bound on the sum of `pattern` on one device may be relied on, other than what follows from the above.
Results may differ from the reference program's by a relative error of at most 0.0076.
Values may be sent and summed in bfloat16 or wider, within the bound.
No kernel may reach another device: no remote copies, remote signals or barrier semaphores. Data moves between devices by JAX's collectives and lax.ppermute only.
A program may use at most 256 MiB of HBM per device.

```python
import math
import jax
import jax.numpy as jnp
from jax import lax

D = 4096
HEADS = 32
DH = 128
BLK = 128
LEVELS = 7
TOKENS = 16384
NBLK = 128
HD = 4096


def query_key_pair(key):
    dims_all = (TOKENS, HEADS * DH)
    query_part = jax.random.truncated_normal(jax.random.fold_in(key, 21), -6.0, 6.0, dims_all, jnp.float32)
    key_part = jax.random.truncated_normal(jax.random.fold_in(key, 22), -6.0, 6.0, dims_all, jnp.float32)
    return (query_part, key_part)


def draw_queries(key, part):
    return query_key_pair(key)[0].astype(jnp.bfloat16)


def draw_key_rows(key, part):
    return query_key_pair(key)[1].astype(jnp.bfloat16)


def place_ends(values, own_key, least, largest):
    spot = [jax.random.randint(jax.random.fold_in(own_key, axis), (), 0, length) for axis, length in enumerate(values.shape)]
    longest = values.shape.index(max(values.shape))
    beside = spot[:longest] + [(spot[longest] + 1) % values.shape[longest]] + spot[longest + 1:]
    return values.at[tuple(spot)].set(least).at[tuple(beside)].set(largest)


def spiked(result, own_key, source, target, parts, factor):
    def block_of(position):
        return (jnp.arange(result.shape[position]) // (result.shape[position] // parts)).reshape((-1,) + (1,) * (result.ndim - 1 - position))

    first = jax.random.permutation(own_key, parts)[block_of(target)]
    second = (block_of(target) + parts // 2) % parts
    return jnp.where((block_of(source) == first) | (block_of(source) == second), factor * result, result)


def block_levels(stream_key, extent, cuts, low, high):
    factor_of, own = 1.0, jax.random.fold_in(stream_key, 6)
    for position, blocks in cuts:
        steps = jnp.exp(jax.random.uniform(jax.random.fold_in(own, position), (blocks,), jnp.float32, low / len(cuts), high / len(cuts)))
        factor_of = factor_of * jnp.repeat(steps, extent[position] // blocks).reshape([-1 if axis == position else 1 for axis in range(len(extent))])
    return factor_of


def bell_draw(rng, extent, scale, most, shards=(), kind=jnp.bfloat16):
    array = scale * jax.random.normal(rng, extent, jnp.float32)
    if shards:
        array = array * block_levels(rng, extent, shards, -0.22, 0.18)
    return jnp.clip(array, -most, most).astype(kind)


def heavy_noise(own_key, dims, spread, most, cuts, heavy, kind=jnp.bfloat16):
    values = spread * jax.random.normal(own_key, dims, jnp.float32)
    if cuts:
        values = values * block_levels(own_key, dims, cuts, -0.22, 0.18)
    return jnp.clip(spiked(values, jax.random.fold_in(own_key, 3), *heavy), -most, most).astype(kind)


def setup_inputs(seed: int = 0) -> dict:
    keys = jax.random.split(jax.random.key(seed), 7)
    queries = draw_queries(jax.random.fold_in(keys[6], 71), 0)
    key_rows = draw_key_rows(jax.random.fold_in(keys[6], 71), 0)
    value_rows = bell_draw(keys[2], (TOKENS, HD), 1.0, 6.0, ((0, 16), (1, 8)))
    out_weight = bell_draw(keys[3], (HD, D), (D // 16) ** -0.5, 0.375, ((0, 8),))
    cotangent = heavy_noise(keys[4], (TOKENS, D), 0.25, 1.5, ((0, 16), (1, 8)), (0, 1, 16, 2.0))
    pattern = place_ends((jax.random.randint(keys[5], (NBLK, LEVELS), 0, 4) < 3).astype(jnp.int32), jax.random.fold_in(keys[5], 1), 0, 1)
    return {"queries": queries, "key_rows": key_rows, "value_rows": value_rows, "out_weight": out_weight, "cotangent": cotangent, "pattern": pattern}


LOG_TWO = math.log(2.0)


def pool_rows(tensor, factor):
    return tensor.astype(jnp.float32).reshape(tensor.shape[0] // factor, factor, tensor.shape[1]).mean(axis=1)


def add_rows(target, start, extra):
    current = lax.dynamic_slice_in_dim(target, start, BLK, 0)
    return lax.dynamic_update_slice_in_dim(target, current + extra, start, 0)


def reference(queries, key_rows, value_rows, out_weight, cotangent, pattern):
    score_scale = DH ** -0.5
    grad_attn = jnp.dot(cotangent, out_weight.T, preferred_element_type=jnp.float32).astype(jnp.bfloat16)
    low_keys = [pool_rows(key_rows, 2 ** level_idx).astype(jnp.bfloat16) for level_idx in range(LEVELS)]
    low_vals = [pool_rows(value_rows, 2 ** level_idx).astype(jnp.bfloat16) for level_idx in range(LEVELS)]
    key_bias = jnp.concatenate([jnp.zeros((BLK,), jnp.float32)] + [jnp.full((BLK,), level_idx * LOG_TWO, jnp.float32) for level_idx in range(LEVELS)])
    keys_all = (1 + LEVELS) * BLK

    def visit(carried, block_idx):
        acc_keys, acc_vals = carried
        first_row = block_idx * BLK
        starts = [first_row] + [jnp.bitwise_xor(jnp.right_shift(block_idx, level_idx), 1) * BLK for level_idx in range(LEVELS)]
        key_set = jnp.concatenate([lax.dynamic_slice_in_dim(key_rows, first_row, BLK, 0)] + [lax.dynamic_slice_in_dim(low_keys[level_idx], starts[level_idx + 1], BLK, 0) for level_idx in range(LEVELS)], axis=0)
        val_set = jnp.concatenate([lax.dynamic_slice_in_dim(value_rows, first_row, BLK, 0)] + [lax.dynamic_slice_in_dim(low_vals[level_idx], starts[level_idx + 1], BLK, 0) for level_idx in range(LEVELS)], axis=0)
        level_flags = lax.dynamic_index_in_dim(pattern, block_idx, 0, keepdims=False) == 1
        kept_mask = jnp.concatenate([jnp.ones((BLK,), bool), jnp.repeat(level_flags, BLK)])
        query_heads = lax.dynamic_slice_in_dim(queries, first_row, BLK, 0).astype(jnp.float32).reshape(BLK, HEADS, DH)
        key_heads = key_set.astype(jnp.float32).reshape(keys_all, HEADS, DH)
        value_heads = val_set.astype(jnp.float32).reshape(keys_all, HEADS, DH)
        grad_heads = lax.dynamic_slice_in_dim(grad_attn, first_row, BLK, 0).astype(jnp.float32).reshape(BLK, HEADS, DH)
        scores = jnp.einsum('qhd,khd->hqk', query_heads, key_heads) * score_scale + key_bias
        scores = jnp.where(kept_mask, scores, -jnp.inf)
        row_max = jnp.max(scores, axis=-1, keepdims=True)
        weights_raw = jnp.exp(scores - row_max)
        attn_prob = weights_raw / jnp.sum(weights_raw, axis=-1, keepdims=True)
        prob_low = lax.optimization_barrier(attn_prob.astype(jnp.bfloat16)).astype(jnp.float32)
        attended_block = jnp.einsum('hqk,khd->qhd', prob_low, value_heads).astype(jnp.bfloat16).reshape(BLK, HD)
        grad_prob = jnp.einsum('qhd,khd->hqk', grad_heads, value_heads)
        row_delta = jnp.sum(attn_prob * grad_prob, axis=-1, keepdims=True)
        grad_score = lax.optimization_barrier((attn_prob * (grad_prob - row_delta)).astype(jnp.bfloat16)).astype(jnp.float32)
        grad_query_block = (jnp.einsum('hqk,khd->qhd', grad_score, key_heads) * score_scale).astype(jnp.bfloat16).reshape(BLK, HD)
        grad_keyset = (jnp.einsum('hqk,qhd->khd', grad_score, query_heads) * score_scale).reshape(keys_all, HD)
        grad_valset = jnp.einsum('hqk,qhd->khd', prob_low, grad_heads).reshape(keys_all, HD)
        acc_keys = list(acc_keys)
        acc_vals = list(acc_vals)
        acc_keys[0] = add_rows(acc_keys[0], first_row, grad_keyset[:BLK])
        acc_vals[0] = add_rows(acc_vals[0], first_row, grad_valset[:BLK])
        for level_idx in range(LEVELS):
            lower = (level_idx + 1) * BLK
            acc_keys[level_idx] = add_rows(acc_keys[level_idx], starts[level_idx + 1], grad_keyset[lower:lower + BLK])
            acc_vals[level_idx] = add_rows(acc_vals[level_idx], starts[level_idx + 1], grad_valset[lower:lower + BLK])
        return (acc_keys, acc_vals), (attended_block, grad_query_block)

    start_keys = [jnp.zeros((TOKENS // 2 ** level_idx, HD), jnp.float32) for level_idx in range(LEVELS)]
    start_vals = [jnp.zeros((TOKENS // 2 ** level_idx, HD), jnp.float32) for level_idx in range(LEVELS)]
    (acc_keys, acc_vals), (attended, grad_query) = lax.scan(visit, (start_keys, start_vals), jnp.arange(NBLK, dtype=jnp.int32))
    attended = attended.reshape(TOKENS, HD)
    grad_query = grad_query.reshape(TOKENS, HD)
    grad_keys = jnp.zeros((TOKENS, HD), jnp.float32)
    grad_values = jnp.zeros((TOKENS, HD), jnp.float32)
    for level_idx in range(LEVELS):
        factor = 2 ** level_idx
        grad_keys = grad_keys + jnp.repeat(acc_keys[level_idx], factor, axis=0) * (1.0 / factor)
        grad_values = grad_values + jnp.repeat(acc_vals[level_idx], factor, axis=0) * (1.0 / factor)
    output = jnp.dot(attended, out_weight, preferred_element_type=jnp.float32).astype(jnp.bfloat16)
    grad_weight = jnp.dot(cotangent.T, attended, preferred_element_type=jnp.float32)
    return output, grad_query, grad_keys.astype(jnp.bfloat16), grad_values.astype(jnp.bfloat16), grad_weight
```

```python
import math

import jax
import jax.numpy as jnp
from jax import lax
from jax.sharding import PartitionSpec as P

DH = 128
BLK = 128


LOG_TWO = math.log(2.0)


def swapped(value, axis, bit):
    mask = 2**bit
    pairs = [(source, source ^ mask) for source in range(lax.axis_size(axis))]
    return lax.ppermute(value, axis, pairs)


def pair_mean(tensor):
    shape_in = tensor.shape
    paired = tensor.reshape(shape_in[:-2] + (shape_in[-2] // 2, 2, shape_in[-1]))
    return jnp.sum(paired, axis=-2) * 0.5


def spread_rows(grads, factor):
    shape_in = grads.shape
    wide = jnp.broadcast_to(grads[..., :, None, :], shape_in[:-1] + (factor, shape_in[-1])) * (
        1.0 / factor
    )
    return wide.reshape(shape_in[:-2] + (shape_in[-2] * factor, shape_in[-1]))


def head_ring_gather(value):
    count = lax.axis_size("head")
    rings = count // 2
    width = value.shape[-1]
    where_head = lax.axis_index("head")
    ring_pos = where_head // 2
    partner = lax.ppermute(value, "head", [(src, src ^ 1) for src in range(count)])
    low_first = where_head % 2 == 0
    pair_block = jnp.concatenate(
        [jnp.where(low_first, value, partner), jnp.where(low_first, partner, value)], axis=-1
    )
    upward = [(src, ((src // 2 + 1) % rings) * 2 + src % 2) for src in range(count)]
    downward = [(src, ((src // 2 - 1) % rings) * 2 + src % 2) for src in range(count)]
    from_below = lax.ppermute(pair_block, "head", upward)
    from_above = lax.ppermute(pair_block, "head", downward)
    blocks = [pair_block, from_above]
    if rings == 4:
        far = jnp.concatenate(
            [
                lax.ppermute(from_below[..., :width], "head", upward),
                lax.ppermute(from_above[..., width:], "head", downward),
            ],
            axis=-1,
        )
        blocks = [pair_block, from_above, far, from_below]
    stacked = jnp.stack(blocks)
    order = (jnp.arange(rings) - ring_pos) % rings
    placed = stacked[order]
    return jnp.moveaxis(placed, 0, -2).reshape(value.shape[:-1] + (rings * 2 * width,))


def weight_columns(out_weight):
    count = lax.axis_size("head")
    where_head = lax.axis_index("head")
    rows, cols = out_weight.shape
    width = cols // count
    pieces = [lax.dynamic_slice_in_dim(out_weight, where_head * width, width, axis=1)]
    for shift in range(1, count):
        outgoing = lax.dynamic_slice_in_dim(
            out_weight, ((where_head + shift) % count) * width, width, axis=1
        )
        pieces.append(
            lax.ppermute(outgoing, "head", [(src, (src + shift) % count) for src in range(count)])
        )
    stacked = jnp.stack(pieces)
    order = (where_head - jnp.arange(count)) % count
    placed = jnp.zeros_like(stacked).at[order].set(stacked)
    return placed.reshape(count * rows, width)


def body(queries, key_rows, value_rows, out_weight, cotangent, pattern):
    row_count, features = queries.shape
    blocks = row_count // BLK
    local_levels = blocks.bit_length() - 1
    seq_count = lax.axis_size("seq")
    cross_levels = seq_count.bit_length() - 1
    level_count = local_levels + cross_levels
    head_count = features // DH
    keys_all = (1 + level_count) * BLK
    score_scale = DH ** (-0.5)
    where_seq = lax.axis_index("seq")
    stacked = jnp.stack([key_rows, value_rows])
    coarse_base = (
        stacked.reshape(2, BLK, row_count // BLK, features).astype(jnp.float32).mean(axis=2)
    )
    siblings = []
    current = coarse_base
    for level_idx in range(cross_levels):
        received = swapped(current, "seq", level_idx)
        siblings.append(received)
        if level_idx + 1 < cross_levels:
            upper_half = jnp.right_shift(where_seq, level_idx) & 1 == 1
            joined = jnp.where(
                upper_half,
                jnp.concatenate([received, current], axis=1),
                jnp.concatenate([current, received], axis=1),
            )
            current = pair_mean(joined)
    segments = [stacked.reshape(2, blocks, BLK, features)]
    for level_idx in range(local_levels):
        factor = 2**level_idx
        group_count = blocks >> level_idx
        if level_idx == 0:
            pooled = stacked
        else:
            pooled = (
                stacked.reshape(2, row_count // factor, factor, features)
                .astype(jnp.float32)
                .mean(axis=2)
                .astype(jnp.bfloat16)
            )
        sibling = pooled.reshape(2, group_count // 2, 2, BLK, features)[:, :, ::-1].reshape(
            2, group_count, BLK, features
        )
        segments.append(
            jnp.broadcast_to(sibling[:, :, None], (2, group_count, factor, BLK, features)).reshape(
                2, blocks, BLK, features
            )
        )
    for level_idx in range(cross_levels):
        segments.append(
            jnp.broadcast_to(
                siblings[level_idx].astype(jnp.bfloat16)[:, None], (2, blocks, BLK, features)
            )
        )
    key_set = jnp.concatenate(segments, axis=2)
    key_bias = jnp.concatenate(
        [jnp.zeros((BLK,), jnp.float32)]
        + [jnp.full((BLK,), level_idx * LOG_TWO, jnp.float32) for level_idx in range(level_count)]
    )
    level_flags = pattern == 1
    kept_mask = jnp.concatenate(
        [
            jnp.ones((blocks, BLK), bool),
            jnp.broadcast_to(level_flags[:, :, None], (blocks, level_count, BLK)).reshape(
                blocks, level_count * BLK
            ),
        ],
        axis=1,
    )
    query_heads = queries.reshape(blocks, BLK, head_count, DH)
    key_heads = key_set[0].reshape(blocks, keys_all, head_count, DH)
    value_heads = key_set[1].reshape(blocks, keys_all, head_count, DH)
    scores = (
        jnp.einsum("bqhd,bkhd->bhqk", query_heads, key_heads, preferred_element_type=jnp.float32)
        * score_scale
        + key_bias
    )
    scores = jnp.where(kept_mask[:, None, None, :], scores, -jnp.inf)
    row_max = jnp.max(scores, axis=-1, keepdims=True)
    weights_raw = jnp.exp(scores - row_max)
    attn_prob = weights_raw / jnp.sum(weights_raw, axis=-1, keepdims=True)
    prob_low = attn_prob.astype(jnp.bfloat16)
    mixed = jnp.einsum("bhqk,bkhd->bqhd", prob_low, value_heads, preferred_element_type=jnp.float32)
    attended = mixed.astype(jnp.bfloat16).reshape(row_count, features)
    attended_full = head_ring_gather(attended)
    output = jnp.dot(
        attended_full, weight_columns(out_weight), preferred_element_type=jnp.float32
    ).astype(jnp.bfloat16)
    grads_full = lax.all_gather(cotangent, "head", axis=1, tiled=True)
    grad_attn = lax.dot_general(
        grads_full, out_weight, (((1,), (1,)), ((), ())), preferred_element_type=jnp.float32
    ).astype(jnp.bfloat16)
    grad_weight = lax.psum_scatter(
        lax.dot_general(
            grads_full, attended, (((0,), (0,)), ((), ())), preferred_element_type=jnp.float32
        ),
        "seq",
        scatter_dimension=0,
        tiled=True,
    )
    grad_heads = grad_attn.reshape(blocks, BLK, head_count, DH)
    grad_prob = jnp.einsum(
        "bqhd,bkhd->bhqk", grad_heads, value_heads, preferred_element_type=jnp.float32
    )
    row_delta = jnp.sum(attn_prob * grad_prob, axis=-1, keepdims=True)
    grad_score = (attn_prob * (grad_prob - row_delta)).astype(jnp.bfloat16)
    grad_query = (
        (
            jnp.einsum("bhqk,bkhd->bqhd", grad_score, key_heads, preferred_element_type=jnp.float32)
            * score_scale
        )
        .astype(jnp.bfloat16)
        .reshape(row_count, features)
    )
    grad_keyset = (
        jnp.einsum("bhqk,bqhd->bkhd", grad_score, query_heads, preferred_element_type=jnp.float32)
        * score_scale
    )
    grad_valset = jnp.einsum(
        "bhqk,bqhd->bkhd", prob_low, grad_heads, preferred_element_type=jnp.float32
    )
    grad_sets = jnp.stack([grad_keyset, grad_valset]).reshape(2, blocks, keys_all, features)
    token_grad = grad_sets[:, :, :BLK].reshape(2, row_count, features)
    for level_idx in range(local_levels):
        factor = 2**level_idx
        group_count = blocks >> level_idx
        lower = (level_idx + 1) * BLK
        segment = (
            grad_sets[:, :, lower : lower + BLK]
            .reshape(2, group_count, factor, BLK, features)
            .sum(axis=2)
        )
        restored = segment.reshape(2, group_count // 2, 2, BLK, features)[:, :, ::-1].reshape(
            2, group_count * BLK, features
        )
        token_grad = token_grad + spread_rows(restored, factor)
    sibling_grads = []
    for level_idx in range(cross_levels):
        lower = (local_levels + 1 + level_idx) * BLK
        sibling_grads.append(jnp.sum(grad_sets[:, :, lower : lower + BLK], axis=1))
    carried = jnp.zeros((2, BLK, features), jnp.float32)
    for level_idx in reversed(range(cross_levels)):
        outgoing = sibling_grads[level_idx]
        if level_idx + 1 < cross_levels:
            halves = spread_rows(carried, 2)
            lower_part = halves[:, :BLK]
            upper_part = halves[:, BLK:]
            upper_half = jnp.right_shift(where_seq, level_idx) & 1 == 1
            own_part = jnp.where(upper_half, upper_part, lower_part)
            outgoing = outgoing + jnp.where(upper_half, lower_part, upper_part)
        else:
            own_part = jnp.zeros_like(outgoing)
        carried = own_part + swapped(outgoing, "seq", level_idx)
    token_grad = token_grad + spread_rows(carried, 2**local_levels)
    grad_keys = token_grad[0].astype(jnp.bfloat16)
    grad_values = token_grad[1].astype(jnp.bfloat16)
    return (output, grad_query, grad_keys, grad_values, grad_weight)


def solution(mesh):
    placed = (
        P("seq", "head"),
        P("seq", "head"),
        P("seq", "head"),
        P("head", None),
        P("seq", "head"),
        P("seq", None),
    )
    return jax.shard_map(
        body,
        mesh=mesh,
        in_specs=placed,
        out_specs=(
            P("seq", "head"),
            P("seq", "head"),
            P("seq", "head"),
            P("seq", "head"),
            P("seq", "head"),
        ),
        check_vma=False,
    )
```

```python
import math

import jax
import jax.numpy as jnp
from jax import lax
from jax.sharding import PartitionSpec as P

DH = 128
BLK = 128


LOG_TWO = math.log(2.0)


def swapped(value, axis, bit):
    mask = 2**bit
    pairs = [(source, source ^ mask) for source in range(lax.axis_size(axis))]
    return lax.ppermute(value, axis, pairs)


def pair_mean(tensor):
    shape_in = tensor.shape
    paired = tensor.reshape(shape_in[:-2] + (shape_in[-2] // 2, 2, shape_in[-1]))
    return jnp.sum(paired, axis=-2) * 0.5


def spread_rows(grads, factor):
    shape_in = grads.shape
    wide = jnp.broadcast_to(grads[..., :, None, :], shape_in[:-1] + (factor, shape_in[-1])) * (
        1.0 / factor
    )
    return wide.reshape(shape_in[:-2] + (shape_in[-2] * factor, shape_in[-1]))


def head_ring_gather(value):
    count = lax.axis_size("head")
    rings = count // 2
    width = value.shape[-1]
    where_head = lax.axis_index("head")
    ring_pos = where_head // 2
    partner = lax.ppermute(value, "head", [(src, src ^ 1) for src in range(count)])
    low_first = where_head % 2 == 0
    pair_block = jnp.concatenate(
        [jnp.where(low_first, value, partner), jnp.where(low_first, partner, value)], axis=-1
    )
    upward = [(src, ((src // 2 + 1) % rings) * 2 + src % 2) for src in range(count)]
    downward = [(src, ((src // 2 - 1) % rings) * 2 + src % 2) for src in range(count)]
    from_below = lax.ppermute(pair_block, "head", upward)
    from_above = lax.ppermute(pair_block, "head", downward)
    blocks = [pair_block, from_above]
    if rings == 4:
        far = jnp.concatenate(
            [
                lax.ppermute(from_below[..., :width], "head", upward),
                lax.ppermute(from_above[..., width:], "head", downward),
            ],
            axis=-1,
        )
        blocks = [pair_block, from_above, far, from_below]
    stacked = jnp.stack(blocks)
    order = (jnp.arange(rings) - ring_pos) % rings
    placed = stacked[order]
    return jnp.moveaxis(placed, 0, -2).reshape(value.shape[:-1] + (rings * 2 * width,))


def weight_columns(out_weight):
    count = lax.axis_size("head")
    where_head = lax.axis_index("head")
    rows, cols = out_weight.shape
    width = cols // count
    pieces = [lax.dynamic_slice_in_dim(out_weight, where_head * width, width, axis=1)]
    for shift in range(1, count):
        outgoing = lax.dynamic_slice_in_dim(
            out_weight, ((where_head + shift) % count) * width, width, axis=1
        )
        pieces.append(
            lax.ppermute(outgoing, "head", [(src, (src + shift) % count) for src in range(count)])
        )
    stacked = jnp.stack(pieces)
    order = (where_head - jnp.arange(count)) % count
    placed = jnp.zeros_like(stacked).at[order].set(stacked)
    return placed.reshape(count * rows, width)


def body(queries, key_rows, value_rows, out_weight, cotangent, pattern):
    row_count, features = queries.shape
    blocks = row_count // BLK
    local_levels = blocks.bit_length() - 1
    seq_count = lax.axis_size("seq")
    cross_levels = seq_count.bit_length() - 1
    level_count = local_levels + cross_levels
    head_count = features // DH
    keys_all = (1 + level_count) * BLK
    score_scale = DH ** (-0.5)
    where_seq = lax.axis_index("seq")
    stacked = jnp.stack([key_rows, value_rows])
    coarse_base = (
        stacked.reshape(2, BLK, row_count // BLK, features).astype(jnp.float32).mean(axis=2)
    )
    siblings = []
    current = coarse_base
    for level_idx in range(cross_levels):
        received = swapped(current, "seq", level_idx)
        siblings.append(received)
        if level_idx + 1 < cross_levels:
            upper_half = jnp.right_shift(where_seq, level_idx) & 1 == 1
            joined = jnp.where(
                upper_half,
                jnp.concatenate([received, current], axis=1),
                jnp.concatenate([current, received], axis=1),
            )
            current = pair_mean(joined)
    segments = [stacked.reshape(2, blocks, BLK, features)]
    for level_idx in range(local_levels):
        factor = 2**level_idx
        group_count = blocks >> level_idx
        if level_idx == 0:
            pooled = stacked
        else:
            pooled = (
                stacked.reshape(2, row_count // factor, factor, features)
                .astype(jnp.float32)
                .mean(axis=2)
                .astype(jnp.bfloat16)
            )
        sibling = pooled.reshape(2, group_count // 2, 2, BLK, features)[:, :, ::-1].reshape(
            2, group_count, BLK, features
        )
        segments.append(
            jnp.broadcast_to(sibling[:, :, None], (2, group_count, factor, BLK, features)).reshape(
                2, blocks, BLK, features
            )
        )
    for level_idx in range(cross_levels):
        segments.append(
            jnp.broadcast_to(
                siblings[level_idx].astype(jnp.bfloat16)[:, None], (2, blocks, BLK, features)
            )
        )
    key_set = jnp.concatenate(segments, axis=2)
    key_bias = jnp.concatenate(
        [jnp.zeros((BLK,), jnp.float32)]
        + [jnp.full((BLK,), level_idx * LOG_TWO, jnp.float32) for level_idx in range(level_count)]
    )
    level_flags = pattern == 1
    kept_mask = jnp.concatenate(
        [
            jnp.ones((blocks, BLK), bool),
            jnp.broadcast_to(level_flags[:, :, None], (blocks, level_count, BLK)).reshape(
                blocks, level_count * BLK
            ),
        ],
        axis=1,
    )
    query_heads = queries.reshape(blocks, BLK, head_count, DH)
    key_heads = key_set[0].reshape(blocks, keys_all, head_count, DH)
    value_heads = key_set[1].reshape(blocks, keys_all, head_count, DH)
    scores = (
        jnp.einsum("bqhd,bkhd->bhqk", query_heads, key_heads, preferred_element_type=jnp.float32)
        * score_scale
        + key_bias
    )
    scores = jnp.where(kept_mask[:, None, None, :], scores, -jnp.inf)
    row_max = jnp.max(scores, axis=-1, keepdims=True)
    weights_raw = jnp.exp(scores - row_max)
    attn_prob = weights_raw / jnp.sum(weights_raw, axis=-1, keepdims=True)
    prob_low = attn_prob.astype(jnp.bfloat16)
    mixed = jnp.einsum("bhqk,bkhd->bqhd", prob_low, value_heads, preferred_element_type=jnp.float32)
    attended = mixed.astype(jnp.bfloat16).reshape(row_count, features)
    half_rows = row_count // 2
    grads_full = jnp.concatenate(
        [
            lax.all_gather(cotangent[:half_rows], "head", axis=1, tiled=True),
            head_ring_gather(cotangent[half_rows:]),
        ],
        axis=0,
    )
    grad_attn = lax.dot_general(
        grads_full, out_weight, (((1,), (1,)), ((), ())), preferred_element_type=jnp.float32
    ).astype(jnp.bfloat16)
    late_attended, late_weight, grad_attn = lax.optimization_barrier(
        (attended, out_weight, grad_attn)
    )
    attended_full = head_ring_gather(late_attended)
    output = jnp.dot(
        attended_full, weight_columns(late_weight), preferred_element_type=jnp.float32
    ).astype(jnp.bfloat16)
    grad_weight = lax.psum_scatter(
        lax.dot_general(
            grads_full, attended, (((0,), (0,)), ((), ())), preferred_element_type=jnp.float32
        ),
        "seq",
        scatter_dimension=0,
        tiled=True,
    )
    grad_heads = grad_attn.reshape(blocks, BLK, head_count, DH)
    grad_prob = jnp.einsum(
        "bqhd,bkhd->bhqk", grad_heads, value_heads, preferred_element_type=jnp.float32
    )
    row_delta = jnp.sum(attn_prob * grad_prob, axis=-1, keepdims=True)
    grad_score = (attn_prob * (grad_prob - row_delta)).astype(jnp.bfloat16)
    grad_query = (
        (
            jnp.einsum("bhqk,bkhd->bqhd", grad_score, key_heads, preferred_element_type=jnp.float32)
            * score_scale
        )
        .astype(jnp.bfloat16)
        .reshape(row_count, features)
    )
    grad_keyset = (
        jnp.einsum("bhqk,bqhd->bkhd", grad_score, query_heads, preferred_element_type=jnp.float32)
        * score_scale
    )
    grad_valset = jnp.einsum(
        "bhqk,bqhd->bkhd", prob_low, grad_heads, preferred_element_type=jnp.float32
    )
    grad_sets = jnp.stack([grad_keyset, grad_valset]).reshape(2, blocks, keys_all, features)
    token_grad = grad_sets[:, :, :BLK].reshape(2, row_count, features)
    for level_idx in range(local_levels):
        factor = 2**level_idx
        group_count = blocks >> level_idx
        lower = (level_idx + 1) * BLK
        segment = (
            grad_sets[:, :, lower : lower + BLK]
            .reshape(2, group_count, factor, BLK, features)
            .sum(axis=2)
        )
        restored = segment.reshape(2, group_count // 2, 2, BLK, features)[:, :, ::-1].reshape(
            2, group_count * BLK, features
        )
        token_grad = token_grad + spread_rows(restored, factor)
    sibling_grads = []
    for level_idx in range(cross_levels):
        lower = (local_levels + 1 + level_idx) * BLK
        sibling_grads.append(jnp.sum(grad_sets[:, :, lower : lower + BLK], axis=1))
    carried = jnp.zeros((2, BLK, features), jnp.float32)
    for level_idx in reversed(range(cross_levels)):
        outgoing = sibling_grads[level_idx]
        if level_idx + 1 < cross_levels:
            halves = spread_rows(carried, 2)
            lower_part = halves[:, :BLK]
            upper_part = halves[:, BLK:]
            upper_half = jnp.right_shift(where_seq, level_idx) & 1 == 1
            own_part = jnp.where(upper_half, upper_part, lower_part)
            outgoing = outgoing + jnp.where(upper_half, lower_part, upper_part)
        else:
            own_part = jnp.zeros_like(outgoing)
        carried = own_part + swapped(outgoing, "seq", level_idx)
    token_grad = token_grad + spread_rows(carried, 2**local_levels)
    grad_keys = token_grad[0].astype(jnp.bfloat16)
    grad_values = token_grad[1].astype(jnp.bfloat16)
    return (output, grad_query, grad_keys, grad_values, grad_weight)


def solution(mesh):
    placed = (
        P("seq", "head"),
        P("seq", "head"),
        P("seq", "head"),
        P("head", None),
        P("seq", "head"),
        P("seq", None),
    )
    return jax.shard_map(
        body,
        mesh=mesh,
        in_specs=placed,
        out_specs=(
            P("seq", "head"),
            P("seq", "head"),
            P("seq", "head"),
            P("seq", "head"),
            P("seq", "head"),
        ),
        check_vma=False,
    )
```

```python
import math

import jax
import jax.numpy as jnp
from jax import lax
from jax.sharding import PartitionSpec as P

DH = 128
BLK = 128


LOG_TWO = math.log(2.0)


def swapped(value, axis, bit):
    mask = 2**bit
    pairs = [(source, source ^ mask) for source in range(lax.axis_size(axis))]
    return lax.ppermute(value, axis, pairs)


def pair_mean(tensor):
    shape_in = tensor.shape
    paired = tensor.reshape(shape_in[:-2] + (shape_in[-2] // 2, 2, shape_in[-1]))
    return jnp.sum(paired, axis=-2) * 0.5


def spread_rows(grads, factor):
    shape_in = grads.shape
    wide = jnp.broadcast_to(grads[..., :, None, :], shape_in[:-1] + (factor, shape_in[-1])) * (
        1.0 / factor
    )
    return wide.reshape(shape_in[:-2] + (shape_in[-2] * factor, shape_in[-1]))


def head_ring_gather(value):
    count = lax.axis_size("head")
    rings = count // 2
    width = value.shape[-1]
    where_head = lax.axis_index("head")
    ring_pos = where_head // 2
    partner = lax.ppermute(value, "head", [(src, src ^ 1) for src in range(count)])
    low_first = where_head % 2 == 0
    pair_block = jnp.concatenate(
        [jnp.where(low_first, value, partner), jnp.where(low_first, partner, value)], axis=-1
    )
    upward = [(src, ((src // 2 + 1) % rings) * 2 + src % 2) for src in range(count)]
    downward = [(src, ((src // 2 - 1) % rings) * 2 + src % 2) for src in range(count)]
    from_below = lax.ppermute(pair_block, "head", upward)
    from_above = lax.ppermute(pair_block, "head", downward)
    blocks = [pair_block, from_above]
    if rings == 4:
        far = jnp.concatenate(
            [
                lax.ppermute(from_below[..., :width], "head", upward),
                lax.ppermute(from_above[..., width:], "head", downward),
            ],
            axis=-1,
        )
        blocks = [pair_block, from_above, far, from_below]
    stacked = jnp.stack(blocks)
    order = (jnp.arange(rings) - ring_pos) % rings
    placed = stacked[order]
    return jnp.moveaxis(placed, 0, -2).reshape(value.shape[:-1] + (rings * 2 * width,))


def weight_columns(out_weight):
    count = lax.axis_size("head")
    seq_count = lax.axis_size("seq")
    where_head = lax.axis_index("head")
    core = lax.axis_index("seq") % 2
    rows, cols = out_weight.shape
    width = cols // count
    own = lax.dynamic_slice_in_dim(out_weight, where_head * width, width, axis=1)
    fetched = []
    for step in range(count // 2):
        shift_low, shift_high = 2 * step + 1, 2 * step + 2
        pairs = []
        for seq_idx in range(seq_count):
            shift = shift_low if seq_idx % 2 == 0 else shift_high
            if shift % count == 0:
                continue
            for src in range(count):
                pairs.append((seq_idx * count + src, seq_idx * count + (src + shift) % count))
        shift = jnp.where(core == 0, shift_low, shift_high)
        outgoing = lax.dynamic_slice_in_dim(
            out_weight, ((where_head + shift) % count) * width, width, axis=1
        )
        fetched.append(lax.ppermute(outgoing, ("seq", "head"), pairs))
    mine = jnp.stack(fetched)
    theirs = lax.ppermute(mine, "seq", [(src, src ^ 1) for src in range(seq_count)])
    odd = jnp.where(core == 0, mine, theirs)
    even = jnp.where(core == 0, theirs, mine)
    by_shift = [own]
    for shift in range(1, count):
        by_shift.append(odd[(shift - 1) // 2] if shift % 2 else even[shift // 2 - 1])
    stacked = jnp.stack(by_shift)
    order = (where_head - jnp.arange(count)) % count
    placed = jnp.zeros_like(stacked).at[order].set(stacked)
    return placed.reshape(count * rows, width)

def body(queries, key_rows, value_rows, out_weight, cotangent, pattern):
    row_count, features = queries.shape
    blocks = row_count // BLK
    local_levels = blocks.bit_length() - 1
    seq_count = lax.axis_size("seq")
    cross_levels = seq_count.bit_length() - 1
    level_count = local_levels + cross_levels
    head_count = features // DH
    keys_all = (1 + level_count) * BLK
    score_scale = DH ** (-0.5)
    where_seq = lax.axis_index("seq")
    stacked = jnp.stack([key_rows, value_rows])
    coarse_base = (
        stacked.reshape(2, BLK, row_count // BLK, features).astype(jnp.float32).mean(axis=2)
    )
    siblings = []
    current = coarse_base
    for level_idx in range(cross_levels):
        received = swapped(current, "seq", level_idx)
        siblings.append(received)
        if level_idx + 1 < cross_levels:
            upper_half = jnp.right_shift(where_seq, level_idx) & 1 == 1
            joined = jnp.where(
                upper_half,
                jnp.concatenate([received, current], axis=1),
                jnp.concatenate([current, received], axis=1),
            )
            current = pair_mean(joined)
    segments = [stacked.reshape(2, blocks, BLK, features)]
    for level_idx in range(local_levels):
        factor = 2**level_idx
        group_count = blocks >> level_idx
        if level_idx == 0:
            pooled = stacked
        else:
            pooled = (
                stacked.reshape(2, row_count // factor, factor, features)
                .astype(jnp.float32)
                .mean(axis=2)
                .astype(jnp.bfloat16)
            )
        sibling = pooled.reshape(2, group_count // 2, 2, BLK, features)[:, :, ::-1].reshape(
            2, group_count, BLK, features
        )
        segments.append(
            jnp.broadcast_to(sibling[:, :, None], (2, group_count, factor, BLK, features)).reshape(
                2, blocks, BLK, features
            )
        )
    for level_idx in range(cross_levels):
        segments.append(
            jnp.broadcast_to(
                siblings[level_idx].astype(jnp.bfloat16)[:, None], (2, blocks, BLK, features)
            )
        )
    key_set = jnp.concatenate(segments, axis=2)
    key_bias = jnp.concatenate(
        [jnp.zeros((BLK,), jnp.float32)]
        + [jnp.full((BLK,), level_idx * LOG_TWO, jnp.float32) for level_idx in range(level_count)]
    )
    level_flags = pattern == 1
    kept_mask = jnp.concatenate(
        [
            jnp.ones((blocks, BLK), bool),
            jnp.broadcast_to(level_flags[:, :, None], (blocks, level_count, BLK)).reshape(
                blocks, level_count * BLK
            ),
        ],
        axis=1,
    )
    query_heads = queries.reshape(blocks, BLK, head_count, DH)
    key_heads = key_set[0].reshape(blocks, keys_all, head_count, DH)
    value_heads = key_set[1].reshape(blocks, keys_all, head_count, DH)
    scores = (
        jnp.einsum("bqhd,bkhd->bhqk", query_heads, key_heads, preferred_element_type=jnp.float32)
        * score_scale
        + key_bias
    )
    scores = jnp.where(kept_mask[:, None, None, :], scores, -jnp.inf)
    row_max = jnp.max(scores, axis=-1, keepdims=True)
    weights_raw = jnp.exp(scores - row_max)
    attn_prob = weights_raw / jnp.sum(weights_raw, axis=-1, keepdims=True)
    prob_low = attn_prob.astype(jnp.bfloat16)
    mixed = jnp.einsum("bhqk,bkhd->bqhd", prob_low, value_heads, preferred_element_type=jnp.float32)
    attended = mixed.astype(jnp.bfloat16).reshape(row_count, features)
    attended, weight_cols = lax.optimization_barrier((attended, weight_columns(out_weight)))
    half_rows = row_count // 2
    grads_full = jnp.concatenate(
        [
            lax.all_gather(cotangent[:half_rows], "head", axis=1, tiled=True),
            head_ring_gather(cotangent[half_rows:]),
        ],
        axis=0,
    )
    grad_attn = lax.dot_general(
        grads_full, out_weight, (((1,), (1,)), ((), ())), preferred_element_type=jnp.float32
    ).astype(jnp.bfloat16)
    late_attended, grad_attn = lax.optimization_barrier((attended, grad_attn))
    attended_full = head_ring_gather(late_attended)
    output = jnp.dot(attended_full, weight_cols, preferred_element_type=jnp.float32).astype(
        jnp.bfloat16
    )
    grad_weight = lax.psum_scatter(
        lax.dot_general(
            grads_full, attended, (((0,), (0,)), ((), ())), preferred_element_type=jnp.float32
        ),
        "seq",
        scatter_dimension=0,
        tiled=True,
    )
    grad_heads = grad_attn.reshape(blocks, BLK, head_count, DH)
    grad_prob = jnp.einsum(
        "bqhd,bkhd->bhqk", grad_heads, value_heads, preferred_element_type=jnp.float32
    )
    row_delta = jnp.sum(attn_prob * grad_prob, axis=-1, keepdims=True)
    grad_score = (attn_prob * (grad_prob - row_delta)).astype(jnp.bfloat16)
    grad_query = (
        (
            jnp.einsum("bhqk,bkhd->bqhd", grad_score, key_heads, preferred_element_type=jnp.float32)
            * score_scale
        )
        .astype(jnp.bfloat16)
        .reshape(row_count, features)
    )
    grad_keyset = (
        jnp.einsum("bhqk,bqhd->bkhd", grad_score, query_heads, preferred_element_type=jnp.float32)
        * score_scale
    )
    grad_valset = jnp.einsum(
        "bhqk,bqhd->bkhd", prob_low, grad_heads, preferred_element_type=jnp.float32
    )
    grad_sets = jnp.stack([grad_keyset, grad_valset]).reshape(2, blocks, keys_all, features)
    token_grad = grad_sets[:, :, :BLK].reshape(2, row_count, features)
    for level_idx in range(local_levels):
        factor = 2**level_idx
        group_count = blocks >> level_idx
        lower = (level_idx + 1) * BLK
        segment = (
            grad_sets[:, :, lower : lower + BLK]
            .reshape(2, group_count, factor, BLK, features)
            .sum(axis=2)
        )
        restored = segment.reshape(2, group_count // 2, 2, BLK, features)[:, :, ::-1].reshape(
            2, group_count * BLK, features
        )
        token_grad = token_grad + spread_rows(restored, factor)
    sibling_grads = []
    for level_idx in range(cross_levels):
        lower = (local_levels + 1 + level_idx) * BLK
        sibling_grads.append(jnp.sum(grad_sets[:, :, lower : lower + BLK], axis=1))
    carried = jnp.zeros((2, BLK, features), jnp.float32)
    for level_idx in reversed(range(cross_levels)):
        outgoing = sibling_grads[level_idx]
        if level_idx + 1 < cross_levels:
            halves = spread_rows(carried, 2)
            lower_part = halves[:, :BLK]
            upper_part = halves[:, BLK:]
            upper_half = jnp.right_shift(where_seq, level_idx) & 1 == 1
            own_part = jnp.where(upper_half, upper_part, lower_part)
            outgoing = outgoing + jnp.where(upper_half, lower_part, upper_part)
        else:
            own_part = jnp.zeros_like(outgoing)
        carried = own_part + swapped(outgoing, "seq", level_idx)
    token_grad = token_grad + spread_rows(carried, 2**local_levels)
    grad_keys = token_grad[0].astype(jnp.bfloat16)
    grad_values = token_grad[1].astype(jnp.bfloat16)
    return (output, grad_query, grad_keys, grad_values, grad_weight)


def solution(mesh):
    placed = (
        P("seq", "head"),
        P("seq", "head"),
        P("seq", "head"),
        P("head", None),
        P("seq", "head"),
        P("seq", None),
    )
    return jax.shard_map(
        body,
        mesh=mesh,
        in_specs=placed,
        out_specs=(
            P("seq", "head"),
            P("seq", "head"),
            P("seq", "head"),
            P("seq", "head"),
            P("seq", "head"),
        ),
        check_vma=False,
    )
```

```python
import math

import jax
import jax.numpy as jnp
from jax import lax
from jax.sharding import PartitionSpec as P

DH = 128
BLK = 128


LOG_TWO = math.log(2.0)


def swapped(value, axis, bit):
    mask = 2**bit
    pairs = [(source, source ^ mask) for source in range(lax.axis_size(axis))]
    return lax.ppermute(value, axis, pairs)


def pair_mean(tensor):
    shape_in = tensor.shape
    paired = tensor.reshape(shape_in[:-2] + (shape_in[-2] // 2, 2, shape_in[-1]))
    return jnp.sum(paired, axis=-2) * 0.5


def spread_rows(grads, factor):
    shape_in = grads.shape
    wide = jnp.broadcast_to(grads[..., :, None, :], shape_in[:-1] + (factor, shape_in[-1])) * (
        1.0 / factor
    )
    return wide.reshape(shape_in[:-2] + (shape_in[-2] * factor, shape_in[-1]))


def head_ring_gather(value, relative=False):
    count = lax.axis_size("head")
    rings = count // 2
    width = value.shape[-1]
    where_head = lax.axis_index("head")
    ring_pos = where_head // 2
    partner = lax.ppermute(value, "head", [(src, src ^ 1) for src in range(count)])
    low_first = where_head % 2 == 0
    pair_block = jnp.concatenate(
        [jnp.where(low_first, value, partner), jnp.where(low_first, partner, value)], axis=-1
    )
    upward = [(src, ((src // 2 + 1) % rings) * 2 + src % 2) for src in range(count)]
    downward = [(src, ((src // 2 - 1) % rings) * 2 + src % 2) for src in range(count)]
    from_below = lax.ppermute(pair_block, "head", upward)
    from_above = lax.ppermute(pair_block, "head", downward)
    blocks = [pair_block, from_above]
    if rings == 4:
        far = jnp.concatenate(
            [
                lax.ppermute(from_below[..., :width], "head", upward),
                lax.ppermute(from_above[..., width:], "head", downward),
            ],
            axis=-1,
        )
        blocks = [pair_block, from_above, far, from_below]
    if relative:
        return blocks
    stacked = jnp.stack(blocks)
    order = (jnp.arange(rings) - ring_pos) % rings
    placed = stacked[order]
    return jnp.moveaxis(placed, 0, -2).reshape(value.shape[:-1] + (rings * 2 * width,))


def weight_columns(out_weight):
    count = lax.axis_size("head")
    seq_count = lax.axis_size("seq")
    where_head = lax.axis_index("head")
    core = lax.axis_index("seq") % 2
    rows, cols = out_weight.shape
    width = cols // count
    own = lax.dynamic_slice_in_dim(out_weight, where_head * width, width, axis=1)
    fetched = []
    for step in range(count // 2):
        shift_low, shift_high = 2 * step + 1, 2 * step + 2
        pairs = []
        for seq_idx in range(seq_count):
            shift = shift_low if seq_idx % 2 == 0 else shift_high
            if shift % count == 0:
                continue
            for src in range(count):
                pairs.append((seq_idx * count + src, seq_idx * count + (src + shift) % count))
        shift = jnp.where(core == 0, shift_low, shift_high)
        outgoing = lax.dynamic_slice_in_dim(
            out_weight, ((where_head + shift) % count) * width, width, axis=1
        )
        fetched.append(lax.ppermute(outgoing, ("seq", "head"), pairs))
    mine = jnp.stack(fetched)
    theirs = lax.ppermute(mine, "seq", [(src, src ^ 1) for src in range(seq_count)])
    odd = jnp.where(core == 0, mine, theirs)
    even = jnp.where(core == 0, theirs, mine)
    by_shift = [own]
    for shift in range(1, count):
        by_shift.append(odd[(shift - 1) // 2] if shift % 2 else even[shift // 2 - 1])
    low_first = where_head % 2 == 0
    ring_blocks = []
    for dist in range(count // 2):
        ring_blocks.append(
            jnp.where(
                low_first,
                jnp.concatenate(
                    [by_shift[(-2 * dist) % count], by_shift[(-1 - 2 * dist) % count]], axis=0
                ),
                jnp.concatenate(
                    [by_shift[(1 - 2 * dist) % count], by_shift[(-2 * dist) % count]], axis=0
                ),
            )
        )
    return ring_blocks

def body(queries, key_rows, value_rows, out_weight, cotangent, pattern):
    row_count, features = queries.shape
    blocks = row_count // BLK
    local_levels = blocks.bit_length() - 1
    seq_count = lax.axis_size("seq")
    cross_levels = seq_count.bit_length() - 1
    level_count = local_levels + cross_levels
    head_count = features // DH
    keys_all = (1 + level_count) * BLK
    score_scale = DH ** (-0.5)
    where_seq = lax.axis_index("seq")
    stacked = jnp.stack([key_rows, value_rows])
    coarse_base = (
        stacked.reshape(2, BLK, row_count // BLK, features).astype(jnp.float32).mean(axis=2)
    )
    siblings = []
    current = coarse_base
    for level_idx in range(cross_levels):
        received = swapped(current, "seq", level_idx)
        siblings.append(received)
        if level_idx + 1 < cross_levels:
            upper_half = jnp.right_shift(where_seq, level_idx) & 1 == 1
            joined = jnp.where(
                upper_half,
                jnp.concatenate([received, current], axis=1),
                jnp.concatenate([current, received], axis=1),
            )
            current = pair_mean(joined)
    segments = [stacked.reshape(2, blocks, BLK, features)]
    for level_idx in range(local_levels):
        factor = 2**level_idx
        group_count = blocks >> level_idx
        if level_idx == 0:
            pooled = stacked
        else:
            pooled = (
                stacked.reshape(2, row_count // factor, factor, features)
                .astype(jnp.float32)
                .mean(axis=2)
                .astype(jnp.bfloat16)
            )
        sibling = pooled.reshape(2, group_count // 2, 2, BLK, features)[:, :, ::-1].reshape(
            2, group_count, BLK, features
        )
        segments.append(
            jnp.broadcast_to(sibling[:, :, None], (2, group_count, factor, BLK, features)).reshape(
                2, blocks, BLK, features
            )
        )
    for level_idx in range(cross_levels):
        segments.append(
            jnp.broadcast_to(
                siblings[level_idx].astype(jnp.bfloat16)[:, None], (2, blocks, BLK, features)
            )
        )
    key_set = jnp.concatenate(segments, axis=2)
    key_bias = jnp.concatenate(
        [jnp.zeros((BLK,), jnp.float32)]
        + [jnp.full((BLK,), level_idx * LOG_TWO, jnp.float32) for level_idx in range(level_count)]
    )
    level_flags = pattern == 1
    kept_mask = jnp.concatenate(
        [
            jnp.ones((blocks, BLK), bool),
            jnp.broadcast_to(level_flags[:, :, None], (blocks, level_count, BLK)).reshape(
                blocks, level_count * BLK
            ),
        ],
        axis=1,
    )
    query_heads = queries.reshape(blocks, BLK, head_count, DH)
    key_heads = key_set[0].reshape(blocks, keys_all, head_count, DH)
    value_heads = key_set[1].reshape(blocks, keys_all, head_count, DH)
    scores = (
        jnp.einsum("bqhd,bkhd->bhqk", query_heads, key_heads, preferred_element_type=jnp.float32)
        * score_scale
        + key_bias
    )
    scores = jnp.where(kept_mask[:, None, None, :], scores, -jnp.inf)
    row_max = jnp.max(scores, axis=-1, keepdims=True)
    weights_raw = jnp.exp(scores - row_max)
    attn_prob = weights_raw / jnp.sum(weights_raw, axis=-1, keepdims=True)
    prob_low = attn_prob.astype(jnp.bfloat16)
    mixed = jnp.einsum("bhqk,bkhd->bqhd", prob_low, value_heads, preferred_element_type=jnp.float32)
    attended = mixed.astype(jnp.bfloat16).reshape(row_count, features)
    attended, weight_cols = lax.optimization_barrier((attended, weight_columns(out_weight)))
    half_rows = row_count // 2
    grads_full = jnp.concatenate(
        [
            lax.all_gather(cotangent[:half_rows], "head", axis=1, tiled=True),
            head_ring_gather(cotangent[half_rows:]),
        ],
        axis=0,
    )
    grad_attn = lax.dot_general(
        grads_full, out_weight, (((1,), (1,)), ((), ())), preferred_element_type=jnp.float32
    ).astype(jnp.bfloat16)
    late_attended, grad_attn = lax.optimization_barrier((attended, grad_attn))
    attended_blocks = head_ring_gather(late_attended, relative=True)
    output_sum = jnp.dot(attended_blocks[0], weight_cols[0], preferred_element_type=jnp.float32)
    for dist in range(1, len(attended_blocks)):
        output_sum = output_sum + jnp.dot(
            attended_blocks[dist], weight_cols[dist], preferred_element_type=jnp.float32
        )
    output = output_sum.astype(jnp.bfloat16)
    grad_weight = lax.psum_scatter(
        lax.dot_general(
            grads_full, attended, (((0,), (0,)), ((), ())), preferred_element_type=jnp.float32
        ),
        "seq",
        scatter_dimension=0,
        tiled=True,
    )
    grad_heads = grad_attn.reshape(blocks, BLK, head_count, DH)
    grad_prob = jnp.einsum(
        "bqhd,bkhd->bhqk", grad_heads, value_heads, preferred_element_type=jnp.float32
    )
    row_delta = jnp.sum(attn_prob * grad_prob, axis=-1, keepdims=True)
    grad_score = (attn_prob * (grad_prob - row_delta)).astype(jnp.bfloat16)
    grad_query = (
        (
            jnp.einsum("bhqk,bkhd->bqhd", grad_score, key_heads, preferred_element_type=jnp.float32)
            * score_scale
        )
        .astype(jnp.bfloat16)
        .reshape(row_count, features)
    )
    grad_keyset = (
        jnp.einsum("bhqk,bqhd->bkhd", grad_score, query_heads, preferred_element_type=jnp.float32)
        * score_scale
    )
    grad_valset = jnp.einsum(
        "bhqk,bqhd->bkhd", prob_low, grad_heads, preferred_element_type=jnp.float32
    )
    grad_sets = jnp.stack([grad_keyset, grad_valset]).reshape(2, blocks, keys_all, features)
    token_grad = grad_sets[:, :, :BLK].reshape(2, row_count, features)
    level_grads = []
    for level_idx in range(local_levels):
        factor = 2**level_idx
        group_count = blocks >> level_idx
        lower = (level_idx + 1) * BLK
        segment = (
            grad_sets[:, :, lower : lower + BLK]
            .reshape(2, group_count, factor, BLK, features)
            .sum(axis=2)
        )
        restored = segment.reshape(2, group_count // 2, 2, BLK, features)[:, :, ::-1].reshape(
            2, group_count * BLK, features
        )
        level_grads.append(restored)
    sibling_grads = []
    for level_idx in range(cross_levels):
        lower = (local_levels + 1 + level_idx) * BLK
        sibling_grads.append(jnp.sum(grad_sets[:, :, lower : lower + BLK], axis=1))
    carried = jnp.zeros((2, BLK, features), jnp.float32)
    for level_idx in reversed(range(cross_levels)):
        outgoing = sibling_grads[level_idx]
        if level_idx + 1 < cross_levels:
            halves = spread_rows(carried, 2)
            lower_part = halves[:, :BLK]
            upper_part = halves[:, BLK:]
            upper_half = jnp.right_shift(where_seq, level_idx) & 1 == 1
            own_part = jnp.where(upper_half, upper_part, lower_part)
            outgoing = outgoing + jnp.where(upper_half, lower_part, upper_part)
        else:
            own_part = jnp.zeros_like(outgoing)
        carried = own_part + swapped(outgoing, "seq", level_idx)
    pooled_grad = carried
    for level_idx in reversed(range(local_levels)):
        pooled_grad = level_grads[level_idx] + spread_rows(pooled_grad, 2)
    token_grad = token_grad + pooled_grad
    grad_keys = token_grad[0].astype(jnp.bfloat16)
    grad_values = token_grad[1].astype(jnp.bfloat16)
    return (output, grad_query, grad_keys, grad_values, grad_weight)


def solution(mesh):
    placed = (
        P("seq", "head"),
        P("seq", "head"),
        P("seq", "head"),
        P("head", None),
        P("seq", "head"),
        P("seq", None),
    )
    return jax.shard_map(
        body,
        mesh=mesh,
        in_specs=placed,
        out_specs=(
            P("seq", "head"),
            P("seq", "head"),
            P("seq", "head"),
            P("seq", "head"),
            P("seq", "head"),
        ),
        check_vma=False,
    )
```

```python
import math

import jax
import jax.numpy as jnp
from jax import lax
from jax.sharding import PartitionSpec as P

DH = 128
BLK = 128


LOG_TWO = math.log(2.0)


def swapped(value, axis, bit):
    mask = 2**bit
    pairs = [(source, source ^ mask) for source in range(lax.axis_size(axis))]
    return lax.ppermute(value, axis, pairs)


def pair_mean(tensor):
    shape_in = tensor.shape
    paired = tensor.reshape(shape_in[:-2] + (shape_in[-2] // 2, 2, shape_in[-1]))
    return jnp.sum(paired, axis=-2) * 0.5


def spread_rows(grads, factor):
    shape_in = grads.shape
    wide = jnp.broadcast_to(grads[..., :, None, :], shape_in[:-1] + (factor, shape_in[-1])) * (
        1.0 / factor
    )
    return wide.reshape(shape_in[:-2] + (shape_in[-2] * factor, shape_in[-1]))


def head_ring_gather(value, relative=False):
    count = lax.axis_size("head")
    rings = count // 2
    width = value.shape[-1]
    where_head = lax.axis_index("head")
    ring_pos = where_head // 2
    partner = lax.ppermute(value, "head", [(src, src ^ 1) for src in range(count)])
    low_first = where_head % 2 == 0
    pair_block = jnp.concatenate(
        [jnp.where(low_first, value, partner), jnp.where(low_first, partner, value)], axis=-1
    )
    upward = [(src, ((src // 2 + 1) % rings) * 2 + src % 2) for src in range(count)]
    downward = [(src, ((src // 2 - 1) % rings) * 2 + src % 2) for src in range(count)]
    from_below = lax.ppermute(pair_block, "head", upward)
    from_above = lax.ppermute(pair_block, "head", downward)
    blocks = [pair_block, from_above]
    if rings == 4:
        far = jnp.concatenate(
            [
                lax.ppermute(from_below[..., :width], "head", upward),
                lax.ppermute(from_above[..., width:], "head", downward),
            ],
            axis=-1,
        )
        blocks = [pair_block, from_above, far, from_below]
    if relative:
        return blocks
    stacked = jnp.stack(blocks)
    order = (jnp.arange(rings) - ring_pos) % rings
    placed = stacked[order]
    return jnp.moveaxis(placed, 0, -2).reshape(value.shape[:-1] + (rings * 2 * width,))


def weight_columns(out_weight):
    count = lax.axis_size("head")
    seq_count = lax.axis_size("seq")
    where_head = lax.axis_index("head")
    core = lax.axis_index("seq") % 2
    rows, cols = out_weight.shape
    width = cols // count
    own = lax.dynamic_slice_in_dim(out_weight, where_head * width, width, axis=1)
    fetched = []
    for step in range(count // 2):
        shift_low, shift_high = 2 * step + 1, 2 * step + 2
        pairs = []
        for seq_idx in range(seq_count):
            shift = shift_low if seq_idx % 2 == 0 else shift_high
            if shift % count == 0:
                continue
            for src in range(count):
                pairs.append((seq_idx * count + src, seq_idx * count + (src + shift) % count))
        shift = jnp.where(core == 0, shift_low, shift_high)
        outgoing = lax.dynamic_slice_in_dim(
            out_weight, ((where_head + shift) % count) * width, width, axis=1
        )
        fetched.append(lax.ppermute(outgoing, ("seq", "head"), pairs))
    mine = jnp.stack(fetched)
    theirs = lax.ppermute(mine, "seq", [(src, src ^ 1) for src in range(seq_count)])
    odd = jnp.where(core == 0, mine, theirs)
    even = jnp.where(core == 0, theirs, mine)
    by_shift = [own]
    for shift in range(1, count):
        by_shift.append(odd[(shift - 1) // 2] if shift % 2 else even[shift // 2 - 1])
    low_first = where_head % 2 == 0
    ring_blocks = []
    for dist in range(count // 2):
        ring_blocks.append(
            jnp.where(
                low_first,
                jnp.concatenate(
                    [by_shift[(-2 * dist) % count], by_shift[(-1 - 2 * dist) % count]], axis=0
                ),
                jnp.concatenate(
                    [by_shift[(1 - 2 * dist) % count], by_shift[(-2 * dist) % count]], axis=0
                ),
            )
        )
    return ring_blocks

def body(queries, key_rows, value_rows, out_weight, cotangent, pattern):
    row_count, features = queries.shape
    blocks = row_count // BLK
    local_levels = blocks.bit_length() - 1
    seq_count = lax.axis_size("seq")
    cross_levels = seq_count.bit_length() - 1
    level_count = local_levels + cross_levels
    head_count = features // DH
    keys_all = (1 + level_count) * BLK
    score_scale = DH ** (-0.5)
    where_seq = lax.axis_index("seq")
    stacked = jnp.stack([key_rows, value_rows])
    coarse_base = (
        stacked.reshape(2, BLK, row_count // BLK, features).astype(jnp.float32).mean(axis=2)
    )
    siblings = []
    current = coarse_base
    for level_idx in range(cross_levels):
        received = swapped(current, "seq", level_idx)
        siblings.append(received)
        if level_idx + 1 < cross_levels:
            upper_half = jnp.right_shift(where_seq, level_idx) & 1 == 1
            joined = jnp.where(
                upper_half,
                jnp.concatenate([received, current], axis=1),
                jnp.concatenate([current, received], axis=1),
            )
            current = pair_mean(joined)
    segments = [stacked.reshape(2, blocks, BLK, features)]
    for level_idx in range(local_levels):
        factor = 2**level_idx
        group_count = blocks >> level_idx
        if level_idx == 0:
            pooled = stacked
        else:
            pooled = (
                stacked.reshape(2, row_count // factor, factor, features)
                .astype(jnp.float32)
                .mean(axis=2)
                .astype(jnp.bfloat16)
            )
        sibling = pooled.reshape(2, group_count // 2, 2, BLK, features)[:, :, ::-1].reshape(
            2, group_count, BLK, features
        )
        segments.append(
            jnp.broadcast_to(sibling[:, :, None], (2, group_count, factor, BLK, features)).reshape(
                2, blocks, BLK, features
            )
        )
    for level_idx in range(cross_levels):
        segments.append(
            jnp.broadcast_to(
                siblings[level_idx].astype(jnp.bfloat16)[:, None], (2, blocks, BLK, features)
            )
        )
    key_set = jnp.concatenate(segments, axis=2)
    key_bias = jnp.concatenate(
        [jnp.zeros((BLK,), jnp.float32)]
        + [jnp.full((BLK,), level_idx * LOG_TWO, jnp.float32) for level_idx in range(level_count)]
    )
    level_flags = pattern == 1
    kept_mask = jnp.concatenate(
        [
            jnp.ones((blocks, BLK), bool),
            jnp.broadcast_to(level_flags[:, :, None], (blocks, level_count, BLK)).reshape(
                blocks, level_count * BLK
            ),
        ],
        axis=1,
    )
    query_heads = queries.reshape(blocks, BLK, head_count, DH)
    key_heads = key_set[0].reshape(blocks, keys_all, head_count, DH)
    value_heads = key_set[1].reshape(blocks, keys_all, head_count, DH)
    scores = (
        jnp.einsum("bqhd,bkhd->bhqk", query_heads, key_heads, preferred_element_type=jnp.float32)
        * score_scale
        + key_bias
    )
    scores = jnp.where(kept_mask[:, None, None, :], scores, -jnp.inf)
    row_max = jnp.max(scores, axis=-1, keepdims=True)
    weights_raw = jnp.exp(scores - row_max)
    attn_prob = weights_raw / jnp.sum(weights_raw, axis=-1, keepdims=True)
    prob_low = attn_prob.astype(jnp.bfloat16)
    mixed = jnp.einsum("bhqk,bkhd->bqhd", prob_low, value_heads, preferred_element_type=jnp.float32)
    attended = mixed.astype(jnp.bfloat16).reshape(row_count, features)
    attended, weight_cols = lax.optimization_barrier((attended, weight_columns(out_weight)))
    half_rows = row_count // 2
    grads_full = jnp.concatenate(
        [
            lax.all_gather(cotangent[:half_rows], "head", axis=1, tiled=True),
            head_ring_gather(cotangent[half_rows:]),
        ],
        axis=0,
    )
    grad_attn = lax.dot_general(
        grads_full, out_weight, (((1,), (1,)), ((), ())), preferred_element_type=jnp.float32
    ).astype(jnp.bfloat16)
    late_attended, grad_attn = lax.optimization_barrier((attended, grad_attn))
    attended_blocks = head_ring_gather(late_attended, relative=True)
    output_sum = jnp.dot(attended_blocks[0], weight_cols[0], preferred_element_type=jnp.float32)
    for dist in range(1, len(attended_blocks)):
        output_sum = output_sum + jnp.dot(
            attended_blocks[dist], weight_cols[dist], preferred_element_type=jnp.float32
        )
    output = output_sum.astype(jnp.bfloat16)
    grad_weight = lax.psum_scatter(
        lax.dot_general(
            grads_full, attended, (((0,), (0,)), ((), ())), preferred_element_type=jnp.float32
        ),
        "seq",
        scatter_dimension=0,
        tiled=True,
    )
    grad_heads = grad_attn.reshape(blocks, BLK, head_count, DH)
    grad_prob = jnp.einsum(
        "bqhd,bkhd->bhqk", grad_heads, value_heads, preferred_element_type=jnp.float32
    )
    row_delta = jnp.sum(attn_prob * grad_prob, axis=-1, keepdims=True)
    grad_score = (attn_prob * (grad_prob - row_delta)).astype(jnp.bfloat16)
    grad_query = (
        (
            jnp.einsum("bhqk,bkhd->bqhd", grad_score, key_heads, preferred_element_type=jnp.float32)
            * score_scale
        )
        .astype(jnp.bfloat16)
        .reshape(row_count, features)
    )
    grad_keyset = (
        jnp.einsum("bhqk,bqhd->bkhd", grad_score, query_heads, preferred_element_type=jnp.float32)
        * score_scale
    )
    grad_valset = jnp.einsum(
        "bhqk,bqhd->bkhd", prob_low, grad_heads, preferred_element_type=jnp.float32
    )
    grad_sets = jnp.stack([grad_keyset, grad_valset]).reshape(2, blocks, keys_all, features)
    token_grad = grad_sets[:, :, :BLK].reshape(2, row_count, features)
    level_grads = []
    for level_idx in range(local_levels):
        factor = 2**level_idx
        group_count = blocks >> level_idx
        lower = (level_idx + 1) * BLK
        segment = (
            grad_sets[:, :, lower : lower + BLK]
            .reshape(2, group_count, factor, BLK, features)
            .sum(axis=2)
        )
        restored = segment.reshape(2, group_count // 2, 2, BLK, features)[:, :, ::-1].reshape(
            2, group_count * BLK, features
        )
        level_grads.append(restored)
    sibling_grads = []
    for level_idx in range(cross_levels):
        lower = (local_levels + 1 + level_idx) * BLK
        sibling_grads.append(jnp.sum(grad_sets[:, :, lower : lower + BLK], axis=1))
    carried = jnp.zeros((2, BLK, features), jnp.float32)
    for level_idx in range(cross_levels):
        group = 2**level_idx
        chunk_rows = BLK // group
        position = where_seq & (group - 1)
        received = None
        for offset in range(group):
            pairs = [
                (src, (((src >> level_idx) ^ 1) << level_idx) + ((src & (group - 1)) ^ offset))
                for src in range(seq_count)
            ]
            piece = lax.dynamic_slice_in_dim(
                sibling_grads[level_idx], (position ^ offset) * chunk_rows, chunk_rows, axis=1
            )
            arrived = lax.ppermute(piece, "seq", pairs)
            received = arrived if received is None else received + arrived
        carried = carried + spread_rows(received, group)
    pooled_grad = carried
    for level_idx in reversed(range(local_levels)):
        pooled_grad = level_grads[level_idx] + spread_rows(pooled_grad, 2)
    token_grad = token_grad + pooled_grad
    grad_keys = token_grad[0].astype(jnp.bfloat16)
    grad_values = token_grad[1].astype(jnp.bfloat16)
    return (output, grad_query, grad_keys, grad_values, grad_weight)


def solution(mesh):
    placed = (
        P("seq", "head"),
        P("seq", "head"),
        P("seq", "head"),
        P("head", None),
        P("seq", "head"),
        P("seq", None),
    )
    return jax.shard_map(
        body,
        mesh=mesh,
        in_specs=placed,
        out_specs=(
            P("seq", "head"),
            P("seq", "head"),
            P("seq", "head"),
            P("seq", "head"),
            P("seq", "head"),
        ),
        check_vma=False,
    )
```

```python
import math

import jax
import jax.numpy as jnp
from jax import lax
from jax.sharding import PartitionSpec as P

DH = 128
BLK = 128


LOG_TWO = math.log(2.0)


def swapped(value, axis, bit):
    mask = 2**bit
    pairs = [(source, source ^ mask) for source in range(lax.axis_size(axis))]
    return lax.ppermute(value, axis, pairs)


def pair_mean(tensor):
    shape_in = tensor.shape
    paired = tensor.reshape(shape_in[:-2] + (shape_in[-2] // 2, 2, shape_in[-1]))
    return jnp.sum(paired, axis=-2) * 0.5


def spread_rows(grads, factor):
    shape_in = grads.shape
    wide = jnp.broadcast_to(grads[..., :, None, :], shape_in[:-1] + (factor, shape_in[-1])) * (
        1.0 / factor
    )
    return wide.reshape(shape_in[:-2] + (shape_in[-2] * factor, shape_in[-1]))


def head_ring_gather(value, relative=False):
    count = lax.axis_size("head")
    rings = count // 2
    width = value.shape[-1]
    where_head = lax.axis_index("head")
    ring_pos = where_head // 2
    partner = lax.ppermute(value, "head", [(src, src ^ 1) for src in range(count)])
    low_first = where_head % 2 == 0
    pair_block = jnp.concatenate(
        [jnp.where(low_first, value, partner), jnp.where(low_first, partner, value)], axis=-1
    )
    upward = [(src, ((src // 2 + 1) % rings) * 2 + src % 2) for src in range(count)]
    downward = [(src, ((src // 2 - 1) % rings) * 2 + src % 2) for src in range(count)]
    from_below = lax.ppermute(pair_block, "head", upward)
    from_above = lax.ppermute(pair_block, "head", downward)
    blocks = [pair_block, from_above]
    if rings == 4:
        far = jnp.concatenate(
            [
                lax.ppermute(from_below[..., :width], "head", upward),
                lax.ppermute(from_above[..., width:], "head", downward),
            ],
            axis=-1,
        )
        blocks = [pair_block, from_above, far, from_below]
    if relative:
        return blocks
    stacked = jnp.stack(blocks)
    order = (jnp.arange(rings) - ring_pos) % rings
    placed = stacked[order]
    return jnp.moveaxis(placed, 0, -2).reshape(value.shape[:-1] + (rings * 2 * width,))


def weight_columns(out_weight):
    count = lax.axis_size("head")
    seq_count = lax.axis_size("seq")
    where_head = lax.axis_index("head")
    core = lax.axis_index("seq") % 2
    rows, cols = out_weight.shape
    width = cols // count
    own = lax.dynamic_slice_in_dim(out_weight, where_head * width, width, axis=1)
    fetched = []
    for step in range(count // 2):
        shift_low, shift_high = 2 * step + 1, 2 * step + 2
        pairs = []
        for seq_idx in range(seq_count):
            shift = shift_low if seq_idx % 2 == 0 else shift_high
            if shift % count == 0:
                continue
            for src in range(count):
                pairs.append((seq_idx * count + src, seq_idx * count + (src + shift) % count))
        shift = jnp.where(core == 0, shift_low, shift_high)
        outgoing = lax.dynamic_slice_in_dim(
            out_weight, ((where_head + shift) % count) * width, width, axis=1
        )
        fetched.append(lax.ppermute(outgoing, ("seq", "head"), pairs))
    mine = jnp.stack(fetched)
    theirs = lax.ppermute(mine, "seq", [(src, src ^ 1) for src in range(seq_count)])
    odd = jnp.where(core == 0, mine, theirs)
    even = jnp.where(core == 0, theirs, mine)
    by_shift = [own]
    for shift in range(1, count):
        by_shift.append(odd[(shift - 1) // 2] if shift % 2 else even[shift // 2 - 1])
    low_first = where_head % 2 == 0
    ring_blocks = []
    for dist in range(count // 2):
        ring_blocks.append(
            jnp.where(
                low_first,
                jnp.concatenate(
                    [by_shift[(-2 * dist) % count], by_shift[(-1 - 2 * dist) % count]], axis=0
                ),
                jnp.concatenate(
                    [by_shift[(1 - 2 * dist) % count], by_shift[(-2 * dist) % count]], axis=0
                ),
            )
        )
    return ring_blocks

def body(queries, key_rows, value_rows, out_weight, cotangent, pattern):
    row_count, features = queries.shape
    blocks = row_count // BLK
    local_levels = blocks.bit_length() - 1
    seq_count = lax.axis_size("seq")
    cross_levels = seq_count.bit_length() - 1
    level_count = local_levels + cross_levels
    head_count = features // DH
    keys_all = (1 + level_count) * BLK
    score_scale = DH ** (-0.5)
    where_seq = lax.axis_index("seq")
    stacked = jnp.stack([key_rows, value_rows])
    coarse_base = (
        stacked.reshape(2, BLK, row_count // BLK, features).astype(jnp.float32).mean(axis=2)
    )
    siblings = []
    current = coarse_base
    for level_idx in range(cross_levels):
        received = swapped(current, "seq", level_idx)
        siblings.append(received)
        if level_idx + 1 < cross_levels:
            upper_half = jnp.right_shift(where_seq, level_idx) & 1 == 1
            joined = jnp.where(
                upper_half,
                jnp.concatenate([received, current], axis=1),
                jnp.concatenate([current, received], axis=1),
            )
            current = pair_mean(joined)
    segments = [stacked.reshape(2, blocks, BLK, features)]
    for level_idx in range(local_levels):
        factor = 2**level_idx
        group_count = blocks >> level_idx
        if level_idx == 0:
            pooled = stacked
        else:
            pooled = (
                stacked.reshape(2, row_count // factor, factor, features)
                .astype(jnp.float32)
                .mean(axis=2)
                .astype(jnp.bfloat16)
            )
        sibling = pooled.reshape(2, group_count // 2, 2, BLK, features)[:, :, ::-1].reshape(
            2, group_count, BLK, features
        )
        segments.append(
            jnp.broadcast_to(sibling[:, :, None], (2, group_count, factor, BLK, features)).reshape(
                2, blocks, BLK, features
            )
        )
    for level_idx in range(cross_levels):
        segments.append(
            jnp.broadcast_to(
                siblings[level_idx].astype(jnp.bfloat16)[:, None], (2, blocks, BLK, features)
            )
        )
    key_set = jnp.concatenate(segments, axis=2)
    key_bias = jnp.concatenate(
        [jnp.zeros((BLK,), jnp.float32)]
        + [jnp.full((BLK,), level_idx * LOG_TWO, jnp.float32) for level_idx in range(level_count)]
    )
    level_flags = pattern == 1
    kept_mask = jnp.concatenate(
        [
            jnp.ones((blocks, BLK), bool),
            jnp.broadcast_to(level_flags[:, :, None], (blocks, level_count, BLK)).reshape(
                blocks, level_count * BLK
            ),
        ],
        axis=1,
    )
    query_heads = queries.reshape(blocks, BLK, head_count, DH)
    key_heads = key_set[0].reshape(blocks, keys_all, head_count, DH)
    value_heads = key_set[1].reshape(blocks, keys_all, head_count, DH)
    scores = (
        jnp.einsum("bqhd,bkhd->bhqk", query_heads, key_heads, preferred_element_type=jnp.float32)
        * score_scale
        + key_bias
    )
    scores = jnp.where(kept_mask[:, None, None, :], scores, -jnp.inf)
    row_max = jnp.max(scores, axis=-1, keepdims=True)
    weights_raw = jnp.exp(scores - row_max)
    attn_prob = weights_raw / jnp.sum(weights_raw, axis=-1, keepdims=True)
    prob_low = attn_prob.astype(jnp.bfloat16)
    mixed = jnp.einsum("bhqk,bkhd->bqhd", prob_low, value_heads, preferred_element_type=jnp.float32)
    attended = mixed.astype(jnp.bfloat16).reshape(row_count, features)
    attended, weight_cols = lax.optimization_barrier((attended, weight_columns(out_weight)))
    half_rows = row_count // 2
    grads_full = jnp.concatenate(
        [
            lax.all_gather(cotangent[:half_rows], "head", axis=1, tiled=True),
            head_ring_gather(cotangent[half_rows:]),
        ],
        axis=0,
    )
    grad_attn = lax.dot_general(
        grads_full, out_weight, (((1,), (1,)), ((), ())), preferred_element_type=jnp.float32
    ).astype(jnp.bfloat16)
    late_attended, grad_attn = lax.optimization_barrier((attended, grad_attn))
    attended_blocks = head_ring_gather(late_attended, relative=True)
    grad_weight = lax.psum_scatter(
        lax.dot_general(
            grads_full, attended, (((0,), (0,)), ((), ())), preferred_element_type=jnp.float32
        ),
        "seq",
        scatter_dimension=0,
        tiled=True,
    )
    grad_heads = grad_attn.reshape(blocks, BLK, head_count, DH)
    grad_prob = jnp.einsum(
        "bqhd,bkhd->bhqk", grad_heads, value_heads, preferred_element_type=jnp.float32
    )
    row_delta = jnp.sum(attn_prob * grad_prob, axis=-1, keepdims=True)
    grad_score = (attn_prob * (grad_prob - row_delta)).astype(jnp.bfloat16)
    grad_query = (
        (
            jnp.einsum("bhqk,bkhd->bqhd", grad_score, key_heads, preferred_element_type=jnp.float32)
            * score_scale
        )
        .astype(jnp.bfloat16)
        .reshape(row_count, features)
    )
    grad_keyset = (
        jnp.einsum("bhqk,bqhd->bkhd", grad_score, query_heads, preferred_element_type=jnp.float32)
        * score_scale
    )
    grad_valset = jnp.einsum(
        "bhqk,bqhd->bkhd", prob_low, grad_heads, preferred_element_type=jnp.float32
    )
    grad_sets = jnp.stack([grad_keyset, grad_valset]).reshape(2, blocks, keys_all, features)
    token_grad = grad_sets[:, :, :BLK].reshape(2, row_count, features)
    level_grads = []
    for level_idx in range(local_levels):
        factor = 2**level_idx
        group_count = blocks >> level_idx
        lower = (level_idx + 1) * BLK
        segment = (
            grad_sets[:, :, lower : lower + BLK]
            .reshape(2, group_count, factor, BLK, features)
            .sum(axis=2)
        )
        restored = segment.reshape(2, group_count // 2, 2, BLK, features)[:, :, ::-1].reshape(
            2, group_count * BLK, features
        )
        level_grads.append(restored)
    sibling_grads = []
    for level_idx in range(cross_levels):
        lower = (local_levels + 1 + level_idx) * BLK
        sibling_grads.append(jnp.sum(grad_sets[:, :, lower : lower + BLK], axis=1))
    carried = jnp.zeros((2, BLK, features), jnp.float32)
    for level_idx in reversed(range(cross_levels)):
        outgoing = sibling_grads[level_idx]
        if level_idx + 1 < cross_levels:
            halves = spread_rows(carried, 2)
            lower_part = halves[:, :BLK]
            upper_part = halves[:, BLK:]
            upper_half = jnp.right_shift(where_seq, level_idx) & 1 == 1
            own_part = jnp.where(upper_half, upper_part, lower_part)
            outgoing = outgoing + jnp.where(upper_half, lower_part, upper_part)
        else:
            own_part = jnp.zeros_like(outgoing)
        carried = own_part + swapped(outgoing, "seq", level_idx)
    attended_blocks, carried = lax.optimization_barrier((attended_blocks, carried))
    output_sum = jnp.dot(attended_blocks[0], weight_cols[0], preferred_element_type=jnp.float32)
    for dist in range(1, len(attended_blocks)):
        output_sum = output_sum + jnp.dot(
            attended_blocks[dist], weight_cols[dist], preferred_element_type=jnp.float32
        )
    output = output_sum.astype(jnp.bfloat16)
    pooled_grad = carried
    for level_idx in reversed(range(local_levels)):
        pooled_grad = level_grads[level_idx] + spread_rows(pooled_grad, 2)
    token_grad = token_grad + pooled_grad
    grad_keys = token_grad[0].astype(jnp.bfloat16)
    grad_values = token_grad[1].astype(jnp.bfloat16)
    return (output, grad_query, grad_keys, grad_values, grad_weight)


def solution(mesh):
    placed = (
        P("seq", "head"),
        P("seq", "head"),
        P("seq", "head"),
        P("head", None),
        P("seq", "head"),
        P("seq", None),
    )
    return jax.shard_map(
        body,
        mesh=mesh,
        in_specs=placed,
        out_specs=(
            P("seq", "head"),
            P("seq", "head"),
            P("seq", "head"),
            P("seq", "head"),
            P("seq", "head"),
        ),
        check_vma=False,
    )
```

```python
import math

import jax
import jax.numpy as jnp
from jax import lax
from jax.sharding import PartitionSpec as P

DH = 128
BLK = 128


LOG_TWO = math.log(2.0)


def swapped(value, axis, bit):
    mask = 2**bit
    pairs = [(source, source ^ mask) for source in range(lax.axis_size(axis))]
    return lax.ppermute(value, axis, pairs)


def pair_mean(tensor):
    shape_in = tensor.shape
    paired = tensor.reshape(shape_in[:-2] + (shape_in[-2] // 2, 2, shape_in[-1]))
    return jnp.sum(paired, axis=-2) * 0.5


def spread_rows(grads, factor):
    shape_in = grads.shape
    wide = jnp.broadcast_to(grads[..., :, None, :], shape_in[:-1] + (factor, shape_in[-1])) * (
        1.0 / factor
    )
    return wide.reshape(shape_in[:-2] + (shape_in[-2] * factor, shape_in[-1]))


def head_ring_gather(value, relative=False):
    count = lax.axis_size("head")
    rings = count // 2
    width = value.shape[-1]
    where_head = lax.axis_index("head")
    ring_pos = where_head // 2
    partner = lax.ppermute(value, "head", [(src, src ^ 1) for src in range(count)])
    low_first = where_head % 2 == 0
    pair_block = jnp.concatenate(
        [jnp.where(low_first, value, partner), jnp.where(low_first, partner, value)], axis=-1
    )
    upward = [(src, ((src // 2 + 1) % rings) * 2 + src % 2) for src in range(count)]
    downward = [(src, ((src // 2 - 1) % rings) * 2 + src % 2) for src in range(count)]
    from_below = lax.ppermute(pair_block, "head", upward)
    from_above = lax.ppermute(pair_block, "head", downward)
    blocks = [pair_block, from_above]
    if rings == 4:
        far = jnp.concatenate(
            [
                lax.ppermute(from_below[..., :width], "head", upward),
                lax.ppermute(from_above[..., width:], "head", downward),
            ],
            axis=-1,
        )
        blocks = [pair_block, from_above, far, from_below]
    if relative:
        return blocks
    stacked = jnp.stack(blocks)
    order = (jnp.arange(rings) - ring_pos) % rings
    placed = stacked[order]
    return jnp.moveaxis(placed, 0, -2).reshape(value.shape[:-1] + (rings * 2 * width,))


def weight_columns(out_weight):
    count = lax.axis_size("head")
    seq_count = lax.axis_size("seq")
    where_head = lax.axis_index("head")
    core = lax.axis_index("seq") % 2
    rows, cols = out_weight.shape
    width = cols // count
    own = lax.dynamic_slice_in_dim(out_weight, where_head * width, width, axis=1)
    fetched = []
    for step in range(count // 2):
        shift_low, shift_high = 2 * step + 1, 2 * step + 2
        pairs = []
        for seq_idx in range(seq_count):
            shift = shift_low if seq_idx % 2 == 0 else shift_high
            if shift % count == 0:
                continue
            for src in range(count):
                pairs.append((seq_idx * count + src, seq_idx * count + (src + shift) % count))
        shift = jnp.where(core == 0, shift_low, shift_high)
        outgoing = lax.dynamic_slice_in_dim(
            out_weight, ((where_head + shift) % count) * width, width, axis=1
        )
        fetched.append(lax.ppermute(outgoing, ("seq", "head"), pairs))
    mine = jnp.stack(fetched)
    theirs = lax.ppermute(mine, "seq", [(src, src ^ 1) for src in range(seq_count)])
    odd = jnp.where(core == 0, mine, theirs)
    even = jnp.where(core == 0, theirs, mine)
    by_shift = [own]
    for shift in range(1, count):
        by_shift.append(odd[(shift - 1) // 2] if shift % 2 else even[shift // 2 - 1])
    low_first = where_head % 2 == 0
    ring_blocks = []
    for dist in range(count // 2):
        ring_blocks.append(
            jnp.where(
                low_first,
                jnp.concatenate(
                    [by_shift[(-2 * dist) % count], by_shift[(-1 - 2 * dist) % count]], axis=0
                ),
                jnp.concatenate(
                    [by_shift[(1 - 2 * dist) % count], by_shift[(-2 * dist) % count]], axis=0
                ),
            )
        )
    return ring_blocks

def body(queries, key_rows, value_rows, out_weight, cotangent, pattern):
    row_count, features = queries.shape
    blocks = row_count // BLK
    local_levels = blocks.bit_length() - 1
    seq_count = lax.axis_size("seq")
    cross_levels = seq_count.bit_length() - 1
    level_count = local_levels + cross_levels
    head_count = features // DH
    keys_all = (1 + level_count) * BLK
    score_scale = DH ** (-0.5)
    where_seq = lax.axis_index("seq")
    stacked = jnp.stack([key_rows, value_rows])
    coarse_base = (
        stacked.reshape(2, BLK, row_count // BLK, features).astype(jnp.float32).mean(axis=2)
    )
    siblings = []
    current = coarse_base
    for level_idx in range(cross_levels):
        received = swapped(current, "seq", level_idx)
        siblings.append(received)
        if level_idx + 1 < cross_levels:
            upper_half = jnp.right_shift(where_seq, level_idx) & 1 == 1
            joined = jnp.where(
                upper_half,
                jnp.concatenate([received, current], axis=1),
                jnp.concatenate([current, received], axis=1),
            )
            current = pair_mean(joined)
    segments = [stacked.reshape(2, blocks, BLK, features)]
    for level_idx in range(local_levels):
        factor = 2**level_idx
        group_count = blocks >> level_idx
        if level_idx == 0:
            pooled = stacked
        else:
            pooled = (
                stacked.reshape(2, row_count // factor, factor, features)
                .astype(jnp.float32)
                .mean(axis=2)
                .astype(jnp.bfloat16)
            )
        sibling = pooled.reshape(2, group_count // 2, 2, BLK, features)[:, :, ::-1].reshape(
            2, group_count, BLK, features
        )
        segments.append(
            jnp.broadcast_to(sibling[:, :, None], (2, group_count, factor, BLK, features)).reshape(
                2, blocks, BLK, features
            )
        )
    key_set = jnp.concatenate(segments, axis=2)
    far_set = jnp.concatenate(
        [siblings[level_idx].astype(jnp.bfloat16) for level_idx in range(cross_levels)], axis=1
    )
    near_keys = (1 + local_levels) * BLK
    far_keys = cross_levels * BLK
    key_bias = jnp.concatenate(
        [jnp.zeros((BLK,), jnp.float32)]
        + [jnp.full((BLK,), level_idx * LOG_TWO, jnp.float32) for level_idx in range(level_count)]
    )
    level_flags = pattern == 1
    kept_mask = jnp.concatenate(
        [
            jnp.ones((blocks, BLK), bool),
            jnp.broadcast_to(level_flags[:, :, None], (blocks, level_count, BLK)).reshape(
                blocks, level_count * BLK
            ),
        ],
        axis=1,
    )
    query_heads = queries.reshape(blocks, BLK, head_count, DH)
    key_heads = key_set[0].reshape(blocks, near_keys, head_count, DH)
    value_heads = key_set[1].reshape(blocks, near_keys, head_count, DH)
    far_key_heads = far_set[0].reshape(far_keys, head_count, DH)
    far_value_heads = far_set[1].reshape(far_keys, head_count, DH)
    scores = (
        jnp.concatenate(
            [
                jnp.einsum(
                    "bqhd,bkhd->bhqk", query_heads, key_heads, preferred_element_type=jnp.float32
                ),
                jnp.einsum(
                    "bqhd,khd->bhqk", query_heads, far_key_heads, preferred_element_type=jnp.float32
                ),
            ],
            axis=-1,
        )
        * score_scale
        + key_bias
    )
    scores = jnp.where(kept_mask[:, None, None, :], scores, -jnp.inf)
    row_max = jnp.max(scores, axis=-1, keepdims=True)
    weights_raw = jnp.exp(scores - row_max)
    attn_prob = weights_raw / jnp.sum(weights_raw, axis=-1, keepdims=True)
    prob_low = attn_prob.astype(jnp.bfloat16)
    near_prob, far_prob = prob_low[..., :near_keys], prob_low[..., near_keys:]
    mixed = jnp.einsum(
        "bhqk,bkhd->bqhd", near_prob, value_heads, preferred_element_type=jnp.float32
    ) + jnp.einsum("bhqk,khd->bqhd", far_prob, far_value_heads, preferred_element_type=jnp.float32)
    attended = mixed.astype(jnp.bfloat16).reshape(row_count, features)
    attended, weight_cols = lax.optimization_barrier((attended, weight_columns(out_weight)))
    half_rows = row_count // 2
    grads_full = jnp.concatenate(
        [
            lax.all_gather(cotangent[:half_rows], "head", axis=1, tiled=True),
            head_ring_gather(cotangent[half_rows:]),
        ],
        axis=0,
    )
    grad_attn = lax.dot_general(
        grads_full, out_weight, (((1,), (1,)), ((), ())), preferred_element_type=jnp.float32
    ).astype(jnp.bfloat16)
    late_attended, grad_attn = lax.optimization_barrier((attended, grad_attn))
    attended_blocks = head_ring_gather(late_attended, relative=True)
    grad_weight = lax.psum_scatter(
        lax.dot_general(
            grads_full, attended, (((0,), (0,)), ((), ())), preferred_element_type=jnp.float32
        ),
        "seq",
        scatter_dimension=0,
        tiled=True,
    )
    grad_heads = grad_attn.reshape(blocks, BLK, head_count, DH)
    grad_prob = jnp.concatenate(
        [
            jnp.einsum(
                "bqhd,bkhd->bhqk", grad_heads, value_heads, preferred_element_type=jnp.float32
            ),
            jnp.einsum(
                "bqhd,khd->bhqk", grad_heads, far_value_heads, preferred_element_type=jnp.float32
            ),
        ],
        axis=-1,
    )
    row_delta = jnp.sum(attn_prob * grad_prob, axis=-1, keepdims=True)
    grad_score = (attn_prob * (grad_prob - row_delta)).astype(jnp.bfloat16)
    near_score, far_score = grad_score[..., :near_keys], grad_score[..., near_keys:]
    grad_query = (
        (
            (
                jnp.einsum(
                    "bhqk,bkhd->bqhd", near_score, key_heads, preferred_element_type=jnp.float32
                )
                + jnp.einsum(
                    "bhqk,khd->bqhd", far_score, far_key_heads, preferred_element_type=jnp.float32
                )
            )
            * score_scale
        )
        .astype(jnp.bfloat16)
        .reshape(row_count, features)
    )
    grad_keyset = (
        jnp.einsum("bhqk,bqhd->bkhd", near_score, query_heads, preferred_element_type=jnp.float32)
        * score_scale
    )
    grad_valset = jnp.einsum(
        "bhqk,bqhd->bkhd", near_prob, grad_heads, preferred_element_type=jnp.float32
    )
    grad_sets = jnp.stack([grad_keyset, grad_valset]).reshape(2, blocks, near_keys, features)
    far_grad_keys = (
        jnp.einsum("bhqk,bqhd->khd", far_score, query_heads, preferred_element_type=jnp.float32)
        * score_scale
    )
    far_grad_values = jnp.einsum(
        "bhqk,bqhd->khd", far_prob, grad_heads, preferred_element_type=jnp.float32
    )
    far_grads = jnp.stack([far_grad_keys, far_grad_values]).reshape(2, far_keys, features)
    token_grad = grad_sets[:, :, :BLK].reshape(2, row_count, features)
    level_grads = []
    for level_idx in range(local_levels):
        factor = 2**level_idx
        group_count = blocks >> level_idx
        lower = (level_idx + 1) * BLK
        segment = (
            grad_sets[:, :, lower : lower + BLK]
            .reshape(2, group_count, factor, BLK, features)
            .sum(axis=2)
        )
        restored = segment.reshape(2, group_count // 2, 2, BLK, features)[:, :, ::-1].reshape(
            2, group_count * BLK, features
        )
        level_grads.append(restored)
    sibling_grads = []
    for level_idx in range(cross_levels):
        sibling_grads.append(far_grads[:, level_idx * BLK : (level_idx + 1) * BLK])
    carried = jnp.zeros((2, BLK, features), jnp.float32)
    for level_idx in reversed(range(cross_levels)):
        outgoing = sibling_grads[level_idx]
        if level_idx + 1 < cross_levels:
            halves = spread_rows(carried, 2)
            lower_part = halves[:, :BLK]
            upper_part = halves[:, BLK:]
            upper_half = jnp.right_shift(where_seq, level_idx) & 1 == 1
            own_part = jnp.where(upper_half, upper_part, lower_part)
            outgoing = outgoing + jnp.where(upper_half, lower_part, upper_part)
        else:
            own_part = jnp.zeros_like(outgoing)
        carried = own_part + swapped(outgoing, "seq", level_idx)
    attended_blocks, carried = lax.optimization_barrier((attended_blocks, carried))
    output_sum = jnp.dot(attended_blocks[0], weight_cols[0], preferred_element_type=jnp.float32)
    for dist in range(1, len(attended_blocks)):
        output_sum = output_sum + jnp.dot(
            attended_blocks[dist], weight_cols[dist], preferred_element_type=jnp.float32
        )
    output = output_sum.astype(jnp.bfloat16)
    pooled_grad = carried
    for level_idx in reversed(range(local_levels)):
        pooled_grad = level_grads[level_idx] + spread_rows(pooled_grad, 2)
    token_grad = token_grad + pooled_grad
    grad_keys = token_grad[0].astype(jnp.bfloat16)
    grad_values = token_grad[1].astype(jnp.bfloat16)
    return (output, grad_query, grad_keys, grad_values, grad_weight)


def solution(mesh):
    placed = (
        P("seq", "head"),
        P("seq", "head"),
        P("seq", "head"),
        P("head", None),
        P("seq", "head"),
        P("seq", None),
    )
    return jax.shard_map(
        body,
        mesh=mesh,
        in_specs=placed,
        out_specs=(
            P("seq", "head"),
            P("seq", "head"),
            P("seq", "head"),
            P("seq", "head"),
            P("seq", "head"),
        ),
        check_vma=False,
    )
```

```python
import math

import jax
import jax.numpy as jnp
from jax import lax
from jax.sharding import PartitionSpec as P

DH = 128
BLK = 128


LOG_TWO = math.log(2.0)


def swapped(value, axis, bit):
    mask = 2**bit
    pairs = [(source, source ^ mask) for source in range(lax.axis_size(axis))]
    return lax.ppermute(value, axis, pairs)


def pair_mean(tensor):
    shape_in = tensor.shape
    paired = tensor.reshape(shape_in[:-2] + (shape_in[-2] // 2, 2, shape_in[-1]))
    return jnp.sum(paired, axis=-2) * 0.5


def spread_rows(grads, factor):
    shape_in = grads.shape
    wide = jnp.broadcast_to(grads[..., :, None, :], shape_in[:-1] + (factor, shape_in[-1])) * (
        1.0 / factor
    )
    return wide.reshape(shape_in[:-2] + (shape_in[-2] * factor, shape_in[-1]))


def head_ring_gather(value, relative=False):
    count = lax.axis_size("head")
    rings = count // 2
    width = value.shape[-1]
    where_head = lax.axis_index("head")
    ring_pos = where_head // 2
    partner = lax.ppermute(value, "head", [(src, src ^ 1) for src in range(count)])
    low_first = where_head % 2 == 0
    pair_block = jnp.concatenate(
        [jnp.where(low_first, value, partner), jnp.where(low_first, partner, value)], axis=-1
    )
    upward = [(src, ((src // 2 + 1) % rings) * 2 + src % 2) for src in range(count)]
    downward = [(src, ((src // 2 - 1) % rings) * 2 + src % 2) for src in range(count)]
    from_below = lax.ppermute(pair_block, "head", upward)
    from_above = lax.ppermute(pair_block, "head", downward)
    blocks = [pair_block, from_above]
    if rings == 4:
        far = jnp.concatenate(
            [
                lax.ppermute(from_below[..., :width], "head", upward),
                lax.ppermute(from_above[..., width:], "head", downward),
            ],
            axis=-1,
        )
        blocks = [pair_block, from_above, far, from_below]
    if relative:
        return blocks
    stacked = jnp.stack(blocks)
    order = (jnp.arange(rings) - ring_pos) % rings
    placed = stacked[order]
    return jnp.moveaxis(placed, 0, -2).reshape(value.shape[:-1] + (rings * 2 * width,))


def weight_columns(out_weight):
    count = lax.axis_size("head")
    seq_count = lax.axis_size("seq")
    where_head = lax.axis_index("head")
    core = lax.axis_index("seq") % 2
    rows, cols = out_weight.shape
    width = cols // count
    own = lax.dynamic_slice_in_dim(out_weight, where_head * width, width, axis=1)
    fetched = []
    for step in range(count // 2):
        shift_low, shift_high = 2 * step + 1, 2 * step + 2
        pairs = []
        for seq_idx in range(seq_count):
            shift = shift_low if seq_idx % 2 == 0 else shift_high
            if shift % count == 0:
                continue
            for src in range(count):
                pairs.append((seq_idx * count + src, seq_idx * count + (src + shift) % count))
        shift = jnp.where(core == 0, shift_low, shift_high)
        outgoing = lax.dynamic_slice_in_dim(
            out_weight, ((where_head + shift) % count) * width, width, axis=1
        )
        fetched.append(lax.ppermute(outgoing, ("seq", "head"), pairs))
    mine = jnp.stack(fetched)
    theirs = lax.ppermute(mine, "seq", [(src, src ^ 1) for src in range(seq_count)])
    odd = jnp.where(core == 0, mine, theirs)
    even = jnp.where(core == 0, theirs, mine)
    by_shift = [own]
    for shift in range(1, count):
        by_shift.append(odd[(shift - 1) // 2] if shift % 2 else even[shift // 2 - 1])
    low_first = where_head % 2 == 0
    ring_blocks = []
    for dist in range(count // 2):
        ring_blocks.append(
            jnp.where(
                low_first,
                jnp.concatenate(
                    [by_shift[(-2 * dist) % count], by_shift[(-1 - 2 * dist) % count]], axis=0
                ),
                jnp.concatenate(
                    [by_shift[(1 - 2 * dist) % count], by_shift[(-2 * dist) % count]], axis=0
                ),
            )
        )
    return ring_blocks

def body(queries, key_rows, value_rows, out_weight, cotangent, pattern):
    row_count, features = queries.shape
    blocks = row_count // BLK
    local_levels = blocks.bit_length() - 1
    seq_count = lax.axis_size("seq")
    cross_levels = seq_count.bit_length() - 1
    level_count = local_levels + cross_levels
    head_count = features // DH
    keys_all = (1 + level_count) * BLK
    score_scale = DH ** (-0.5)
    where_seq = lax.axis_index("seq")
    stacked = jnp.stack([key_rows, value_rows])
    coarse_base = (
        stacked.reshape(2, BLK, row_count // BLK, features).astype(jnp.float32).mean(axis=2)
    )
    siblings = []
    current = coarse_base
    for level_idx in range(cross_levels):
        received = swapped(current, "seq", level_idx)
        siblings.append(received)
        if level_idx + 1 < cross_levels:
            upper_half = jnp.right_shift(where_seq, level_idx) & 1 == 1
            joined = jnp.where(
                upper_half,
                jnp.concatenate([received, current], axis=1),
                jnp.concatenate([current, received], axis=1),
            )
            current = pair_mean(joined)
    per_block = [stacked.reshape(2, blocks, BLK, features)]
    groups = []
    for level_idx in range(local_levels):
        factor = 2**level_idx
        group_count = blocks >> level_idx
        if level_idx == 0:
            pooled = stacked
        else:
            pooled = (
                stacked.reshape(2, row_count // factor, factor, features)
                .astype(jnp.float32)
                .mean(axis=2)
                .astype(jnp.bfloat16)
            )
        sibling = pooled.reshape(2, group_count // 2, 2, BLK, features)[:, :, ::-1].reshape(
            2, group_count, BLK, features
        )
        if factor == 1:
            per_block.append(sibling)
        else:
            groups.append((sibling, factor))
    groups.insert(0, (jnp.concatenate(per_block, axis=2), 1))
    if cross_levels:
        far_set = jnp.concatenate(
            [siblings[level_idx].astype(jnp.bfloat16) for level_idx in range(cross_levels)], axis=1
        )
        groups.append((far_set[:, None], blocks))
    key_groups = [
        (
            rows[0].reshape(rows.shape[1], rows.shape[2], head_count, DH),
            rows[1].reshape(rows.shape[1], rows.shape[2], head_count, DH),
            factor,
        )
        for rows, factor in groups
    ]
    widths = [rows.shape[2] for rows, _ in groups]
    bounds = [sum(widths[:idx]) for idx in range(len(widths) + 1)]

    def by_block(tensor, factor):
        return tensor.reshape((blocks // factor, factor) + tensor.shape[1:])

    def split_keys(tensor):
        return [tensor[..., bounds[idx] : bounds[idx + 1]] for idx in range(len(widths))]

    def against_keys(rows_heads, which):
        parts = []
        for group_keys, group_values, factor in key_groups:
            operand = group_keys if which == 0 else group_values
            part = jnp.einsum(
                "gfqhd,gkhd->gfhqk",
                by_block(rows_heads, factor),
                operand,
                preferred_element_type=jnp.float32,
            )
            parts.append(part.reshape((blocks,) + part.shape[2:]))
        return jnp.concatenate(parts, axis=-1)

    def mix_keys(weights, which):
        total = None
        for (group_keys, group_values, factor), piece in zip(key_groups, split_keys(weights)):
            operand = group_keys if which == 0 else group_values
            part = jnp.einsum(
                "gfhqk,gkhd->gfqhd",
                by_block(piece, factor),
                operand,
                preferred_element_type=jnp.float32,
            ).reshape(blocks, BLK, head_count, DH)
            total = part if total is None else total + part
        return total

    def key_grads(weights, rows_heads):
        out = []
        for (_, _, factor), piece in zip(key_groups, split_keys(weights)):
            out.append(
                jnp.einsum(
                    "gfhqk,gfqhd->gkhd",
                    by_block(piece, factor),
                    by_block(rows_heads, factor),
                    preferred_element_type=jnp.float32,
                )
            )
        return out

    key_bias = jnp.concatenate(
        [jnp.zeros((BLK,), jnp.float32)]
        + [jnp.full((BLK,), level_idx * LOG_TWO, jnp.float32) for level_idx in range(level_count)]
    )
    level_flags = pattern == 1
    kept_mask = jnp.concatenate(
        [
            jnp.ones((blocks, BLK), bool),
            jnp.broadcast_to(level_flags[:, :, None], (blocks, level_count, BLK)).reshape(
                blocks, level_count * BLK
            ),
        ],
        axis=1,
    )
    query_heads = queries.reshape(blocks, BLK, head_count, DH)
    scores = against_keys(query_heads, 0) * score_scale + key_bias
    scores = jnp.where(kept_mask[:, None, None, :], scores, -jnp.inf)
    row_max = jnp.max(scores, axis=-1, keepdims=True)
    weights_raw = jnp.exp(scores - row_max)
    attn_prob = weights_raw / jnp.sum(weights_raw, axis=-1, keepdims=True)
    prob_low = attn_prob.astype(jnp.bfloat16)
    mixed = mix_keys(prob_low, 1)
    attended = mixed.astype(jnp.bfloat16).reshape(row_count, features)
    attended, weight_cols = lax.optimization_barrier((attended, weight_columns(out_weight)))
    half_rows = row_count // 2
    grads_full = jnp.concatenate(
        [
            lax.all_gather(cotangent[:half_rows], "head", axis=1, tiled=True),
            head_ring_gather(cotangent[half_rows:]),
        ],
        axis=0,
    )
    grad_attn = lax.dot_general(
        grads_full, out_weight, (((1,), (1,)), ((), ())), preferred_element_type=jnp.float32
    ).astype(jnp.bfloat16)
    late_attended, grad_attn = lax.optimization_barrier((attended, grad_attn))
    attended_blocks = head_ring_gather(late_attended, relative=True)
    grad_weight = lax.psum_scatter(
        lax.dot_general(
            grads_full, attended, (((0,), (0,)), ((), ())), preferred_element_type=jnp.float32
        ),
        "seq",
        scatter_dimension=0,
        tiled=True,
    )
    grad_heads = grad_attn.reshape(blocks, BLK, head_count, DH)
    grad_prob = against_keys(grad_heads, 1)
    row_delta = jnp.sum(attn_prob * grad_prob, axis=-1, keepdims=True)
    grad_score = (attn_prob * (grad_prob - row_delta)).astype(jnp.bfloat16)
    grad_query = (
        (mix_keys(grad_score, 0) * score_scale).astype(jnp.bfloat16).reshape(row_count, features)
    )
    grad_groups = [
        jnp.stack([keys_part * score_scale, values_part]).reshape(
            (2,) + keys_part.shape[:2] + (features,)
        )
        for keys_part, values_part in zip(
            key_grads(grad_score, query_heads), key_grads(prob_low, grad_heads)
        )
    ]
    near = grad_groups[0]
    token_grad = near[:, :, :BLK].reshape(2, row_count, features)
    level_grads = []
    for level_idx in range(local_levels):
        group_count = blocks >> level_idx
        if level_idx == 0:
            segment = near[:, :, BLK : 2 * BLK]
        else:
            segment = grad_groups[level_idx][:, :, :BLK]
        restored = segment.reshape(2, group_count // 2, 2, BLK, features)[:, :, ::-1].reshape(
            2, group_count * BLK, features
        )
        level_grads.append(restored)
    sibling_grads = []
    if cross_levels:
        far_grads = grad_groups[-1][:, 0]
        for level_idx in range(cross_levels):
            sibling_grads.append(far_grads[:, level_idx * BLK : (level_idx + 1) * BLK])
    carried = jnp.zeros((2, BLK, features), jnp.float32)
    for level_idx in reversed(range(cross_levels)):
        outgoing = sibling_grads[level_idx]
        if level_idx + 1 < cross_levels:
            halves = spread_rows(carried, 2)
            lower_part = halves[:, :BLK]
            upper_part = halves[:, BLK:]
            upper_half = jnp.right_shift(where_seq, level_idx) & 1 == 1
            own_part = jnp.where(upper_half, upper_part, lower_part)
            outgoing = outgoing + jnp.where(upper_half, lower_part, upper_part)
        else:
            own_part = jnp.zeros_like(outgoing)
        carried = own_part + swapped(outgoing, "seq", level_idx)
    attended_blocks, carried = lax.optimization_barrier((attended_blocks, carried))
    output_sum = jnp.dot(attended_blocks[0], weight_cols[0], preferred_element_type=jnp.float32)
    for dist in range(1, len(attended_blocks)):
        output_sum = output_sum + jnp.dot(
            attended_blocks[dist], weight_cols[dist], preferred_element_type=jnp.float32
        )
    output = output_sum.astype(jnp.bfloat16)
    pooled_grad = carried
    for level_idx in reversed(range(local_levels)):
        pooled_grad = level_grads[level_idx] + spread_rows(pooled_grad, 2)
    token_grad = token_grad + pooled_grad
    grad_keys = token_grad[0].astype(jnp.bfloat16)
    grad_values = token_grad[1].astype(jnp.bfloat16)
    return (output, grad_query, grad_keys, grad_values, grad_weight)


def solution(mesh):
    placed = (
        P("seq", "head"),
        P("seq", "head"),
        P("seq", "head"),
        P("head", None),
        P("seq", "head"),
        P("seq", None),
    )
    return jax.shard_map(
        body,
        mesh=mesh,
        in_specs=placed,
        out_specs=(
            P("seq", "head"),
            P("seq", "head"),
            P("seq", "head"),
            P("seq", "head"),
            P("seq", "head"),
        ),
        check_vma=False,
    )
```

```python
import math

import jax
import jax.numpy as jnp
from jax import lax
from jax.sharding import PartitionSpec as P

DH = 128
BLK = 128


LOG_TWO = math.log(2.0)


def swapped(value, axis, bit):
    mask = 2**bit
    pairs = [(source, source ^ mask) for source in range(lax.axis_size(axis))]
    return lax.ppermute(value, axis, pairs)


def pair_mean(tensor):
    shape_in = tensor.shape
    paired = tensor.reshape(shape_in[:-2] + (shape_in[-2] // 2, 2, shape_in[-1]))
    return jnp.sum(paired, axis=-2) * 0.5


def spread_rows(grads, factor):
    shape_in = grads.shape
    wide = jnp.broadcast_to(grads[..., :, None, :], shape_in[:-1] + (factor, shape_in[-1])) * (
        1.0 / factor
    )
    return wide.reshape(shape_in[:-2] + (shape_in[-2] * factor, shape_in[-1]))


def head_ring_gather(value, relative=False):
    count = lax.axis_size("head")
    rings = count // 2
    width = value.shape[-1]
    where_head = lax.axis_index("head")
    ring_pos = where_head // 2
    partner = lax.ppermute(value, "head", [(src, src ^ 1) for src in range(count)])
    low_first = where_head % 2 == 0
    pair_block = jnp.concatenate(
        [jnp.where(low_first, value, partner), jnp.where(low_first, partner, value)], axis=-1
    )
    upward = [(src, ((src // 2 + 1) % rings) * 2 + src % 2) for src in range(count)]
    downward = [(src, ((src // 2 - 1) % rings) * 2 + src % 2) for src in range(count)]
    from_below = lax.ppermute(pair_block, "head", upward)
    from_above = lax.ppermute(pair_block, "head", downward)
    blocks = [pair_block, from_above]
    if rings == 4:
        far = jnp.concatenate(
            [
                lax.ppermute(from_below[..., :width], "head", upward),
                lax.ppermute(from_above[..., width:], "head", downward),
            ],
            axis=-1,
        )
        blocks = [pair_block, from_above, far, from_below]
    if relative:
        return blocks
    stacked = jnp.stack(blocks)
    order = (jnp.arange(rings) - ring_pos) % rings
    placed = stacked[order]
    return jnp.moveaxis(placed, 0, -2).reshape(value.shape[:-1] + (rings * 2 * width,))


def weight_columns(out_weight):
    count = lax.axis_size("head")
    seq_count = lax.axis_size("seq")
    where_head = lax.axis_index("head")
    core = lax.axis_index("seq") % 2
    rows, cols = out_weight.shape
    width = cols // count
    own = lax.dynamic_slice_in_dim(out_weight, where_head * width, width, axis=1)
    fetched = []
    for step in range(count // 2):
        shift_low, shift_high = 2 * step + 1, 2 * step + 2
        pairs = []
        for seq_idx in range(seq_count):
            shift = shift_low if seq_idx % 2 == 0 else shift_high
            if shift % count == 0:
                continue
            for src in range(count):
                pairs.append((seq_idx * count + src, seq_idx * count + (src + shift) % count))
        shift = jnp.where(core == 0, shift_low, shift_high)
        outgoing = lax.dynamic_slice_in_dim(
            out_weight, ((where_head + shift) % count) * width, width, axis=1
        )
        fetched.append(lax.ppermute(outgoing, ("seq", "head"), pairs))
    mine = jnp.stack(fetched)
    theirs = lax.ppermute(mine, "seq", [(src, src ^ 1) for src in range(seq_count)])
    odd = jnp.where(core == 0, mine, theirs)
    even = jnp.where(core == 0, theirs, mine)
    by_shift = [own]
    for shift in range(1, count):
        by_shift.append(odd[(shift - 1) // 2] if shift % 2 else even[shift // 2 - 1])
    low_first = where_head % 2 == 0
    ring_blocks = []
    for dist in range(count // 2):
        ring_blocks.append(
            jnp.where(
                low_first,
                jnp.concatenate(
                    [by_shift[(-2 * dist) % count], by_shift[(-1 - 2 * dist) % count]], axis=0
                ),
                jnp.concatenate(
                    [by_shift[(1 - 2 * dist) % count], by_shift[(-2 * dist) % count]], axis=0
                ),
            )
        )
    return ring_blocks

def body(queries, key_rows, value_rows, out_weight, cotangent, pattern):
    row_count, features = queries.shape
    blocks = row_count // BLK
    local_levels = blocks.bit_length() - 1
    seq_count = lax.axis_size("seq")
    cross_levels = seq_count.bit_length() - 1
    level_count = local_levels + cross_levels
    head_count = features // DH
    keys_all = (1 + level_count) * BLK
    score_scale = DH ** (-0.5)
    where_seq = lax.axis_index("seq")
    stacked = jnp.stack([key_rows, value_rows])
    coarse_base = (
        stacked.reshape(2, BLK, row_count // BLK, features).astype(jnp.float32).mean(axis=2)
    )
    siblings = []
    current = coarse_base
    for level_idx in range(cross_levels):
        received = swapped(current, "seq", level_idx)
        siblings.append(received)
        if level_idx + 1 < cross_levels:
            upper_half = jnp.right_shift(where_seq, level_idx) & 1 == 1
            joined = jnp.where(
                upper_half,
                jnp.concatenate([received, current], axis=1),
                jnp.concatenate([current, received], axis=1),
            )
            current = pair_mean(joined)
    segments = [stacked.reshape(2, blocks, BLK, features)]
    for level_idx in range(local_levels):
        factor = 2**level_idx
        group_count = blocks >> level_idx
        if level_idx == 0:
            pooled = stacked
        else:
            pooled = (
                stacked.reshape(2, row_count // factor, factor, features)
                .astype(jnp.float32)
                .mean(axis=2)
                .astype(jnp.bfloat16)
            )
        sibling = pooled.reshape(2, group_count // 2, 2, BLK, features)[:, :, ::-1].reshape(
            2, group_count, BLK, features
        )
        segments.append(
            jnp.broadcast_to(sibling[:, :, None], (2, group_count, factor, BLK, features)).reshape(
                2, blocks, BLK, features
            )
        )
    key_set = jnp.concatenate(segments, axis=2)
    far_set = jnp.concatenate(
        [siblings[level_idx].astype(jnp.bfloat16) for level_idx in range(cross_levels)], axis=1
    )
    near_keys = (1 + local_levels) * BLK
    far_keys = cross_levels * BLK
    key_bias = jnp.concatenate(
        [jnp.zeros((BLK,), jnp.float32)]
        + [jnp.full((BLK,), level_idx * LOG_TWO, jnp.float32) for level_idx in range(level_count)]
    )
    level_flags = pattern == 1
    kept_mask = jnp.concatenate(
        [
            jnp.ones((blocks, BLK), bool),
            jnp.broadcast_to(level_flags[:, :, None], (blocks, level_count, BLK)).reshape(
                blocks, level_count * BLK
            ),
        ],
        axis=1,
    )
    half_rows = row_count // 2
    early_half = lax.all_gather(cotangent[:half_rows], "head", axis=1, tiled=True)
    early_half, queries = lax.optimization_barrier((early_half, queries))
    query_heads = queries.reshape(blocks, BLK, head_count, DH)
    key_heads = key_set[0].reshape(blocks, near_keys, head_count, DH)
    value_heads = key_set[1].reshape(blocks, near_keys, head_count, DH)
    far_key_heads = far_set[0].reshape(far_keys, head_count, DH)
    far_value_heads = far_set[1].reshape(far_keys, head_count, DH)
    scores = (
        jnp.concatenate(
            [
                jnp.einsum(
                    "bqhd,bkhd->bhqk", query_heads, key_heads, preferred_element_type=jnp.float32
                ),
                jnp.einsum(
                    "bqhd,khd->bhqk", query_heads, far_key_heads, preferred_element_type=jnp.float32
                ),
            ],
            axis=-1,
        )
        * score_scale
        + key_bias
    )
    scores = jnp.where(kept_mask[:, None, None, :], scores, -jnp.inf)
    row_max = jnp.max(scores, axis=-1, keepdims=True)
    weights_raw = jnp.exp(scores - row_max)
    attn_prob = weights_raw / jnp.sum(weights_raw, axis=-1, keepdims=True)
    prob_low = attn_prob.astype(jnp.bfloat16)
    near_prob, far_prob = prob_low[..., :near_keys], prob_low[..., near_keys:]
    mixed = jnp.einsum(
        "bhqk,bkhd->bqhd", near_prob, value_heads, preferred_element_type=jnp.float32
    ) + jnp.einsum("bhqk,khd->bqhd", far_prob, far_value_heads, preferred_element_type=jnp.float32)
    attended = mixed.astype(jnp.bfloat16).reshape(row_count, features)
    attended, weight_cols = lax.optimization_barrier((attended, weight_columns(out_weight)))
    grads_full = jnp.concatenate([early_half, head_ring_gather(cotangent[half_rows:])], axis=0)
    grad_attn = lax.dot_general(
        grads_full, out_weight, (((1,), (1,)), ((), ())), preferred_element_type=jnp.float32
    ).astype(jnp.bfloat16)
    late_attended, grad_attn = lax.optimization_barrier((attended, grad_attn))
    attended_blocks = head_ring_gather(late_attended, relative=True)
    grad_weight = lax.psum_scatter(
        lax.dot_general(
            grads_full, attended, (((0,), (0,)), ((), ())), preferred_element_type=jnp.float32
        ),
        "seq",
        scatter_dimension=0,
        tiled=True,
    )
    grad_heads = grad_attn.reshape(blocks, BLK, head_count, DH)
    grad_prob = jnp.concatenate(
        [
            jnp.einsum(
                "bqhd,bkhd->bhqk", grad_heads, value_heads, preferred_element_type=jnp.float32
            ),
            jnp.einsum(
                "bqhd,khd->bhqk", grad_heads, far_value_heads, preferred_element_type=jnp.float32
            ),
        ],
        axis=-1,
    )
    row_delta = jnp.sum(attn_prob * grad_prob, axis=-1, keepdims=True)
    grad_score = (attn_prob * (grad_prob - row_delta)).astype(jnp.bfloat16)
    near_score, far_score = grad_score[..., :near_keys], grad_score[..., near_keys:]
    grad_query = (
        (
            (
                jnp.einsum(
                    "bhqk,bkhd->bqhd", near_score, key_heads, preferred_element_type=jnp.float32
                )
                + jnp.einsum(
                    "bhqk,khd->bqhd", far_score, far_key_heads, preferred_element_type=jnp.float32
                )
            )
            * score_scale
        )
        .astype(jnp.bfloat16)
        .reshape(row_count, features)
    )
    grad_keyset = (
        jnp.einsum("bhqk,bqhd->bkhd", near_score, query_heads, preferred_element_type=jnp.float32)
        * score_scale
    )
    grad_valset = jnp.einsum(
        "bhqk,bqhd->bkhd", near_prob, grad_heads, preferred_element_type=jnp.float32
    )
    grad_sets = jnp.stack([grad_keyset, grad_valset]).reshape(2, blocks, near_keys, features)
    far_grad_keys = (
        jnp.einsum("bhqk,bqhd->khd", far_score, query_heads, preferred_element_type=jnp.float32)
        * score_scale
    )
    far_grad_values = jnp.einsum(
        "bhqk,bqhd->khd", far_prob, grad_heads, preferred_element_type=jnp.float32
    )
    far_grads = jnp.stack([far_grad_keys, far_grad_values]).reshape(2, far_keys, features)
    token_grad = grad_sets[:, :, :BLK].reshape(2, row_count, features)
    level_grads = []
    for level_idx in range(local_levels):
        factor = 2**level_idx
        group_count = blocks >> level_idx
        lower = (level_idx + 1) * BLK
        segment = (
            grad_sets[:, :, lower : lower + BLK]
            .reshape(2, group_count, factor, BLK, features)
            .sum(axis=2)
        )
        restored = segment.reshape(2, group_count // 2, 2, BLK, features)[:, :, ::-1].reshape(
            2, group_count * BLK, features
        )
        level_grads.append(restored)
    sibling_grads = []
    for level_idx in range(cross_levels):
        sibling_grads.append(far_grads[:, level_idx * BLK : (level_idx + 1) * BLK])
    carried = jnp.zeros((2, BLK, features), jnp.float32)
    for level_idx in reversed(range(cross_levels)):
        outgoing = sibling_grads[level_idx]
        if level_idx + 1 < cross_levels:
            halves = spread_rows(carried, 2)
            lower_part = halves[:, :BLK]
            upper_part = halves[:, BLK:]
            upper_half = jnp.right_shift(where_seq, level_idx) & 1 == 1
            own_part = jnp.where(upper_half, upper_part, lower_part)
            outgoing = outgoing + jnp.where(upper_half, lower_part, upper_part)
        else:
            own_part = jnp.zeros_like(outgoing)
        carried = own_part + swapped(outgoing, "seq", level_idx)
    attended_blocks, carried = lax.optimization_barrier((attended_blocks, carried))
    output_sum = jnp.dot(attended_blocks[0], weight_cols[0], preferred_element_type=jnp.float32)
    for dist in range(1, len(attended_blocks)):
        output_sum = output_sum + jnp.dot(
            attended_blocks[dist], weight_cols[dist], preferred_element_type=jnp.float32
        )
    output = output_sum.astype(jnp.bfloat16)
    pooled_grad = carried
    for level_idx in reversed(range(local_levels)):
        pooled_grad = level_grads[level_idx] + spread_rows(pooled_grad, 2)
    token_grad = token_grad + pooled_grad
    grad_keys = token_grad[0].astype(jnp.bfloat16)
    grad_values = token_grad[1].astype(jnp.bfloat16)
    return (output, grad_query, grad_keys, grad_values, grad_weight)


def solution(mesh):
    placed = (
        P("seq", "head"),
        P("seq", "head"),
        P("seq", "head"),
        P("head", None),
        P("seq", "head"),
        P("seq", None),
    )
    return jax.shard_map(
        body,
        mesh=mesh,
        in_specs=placed,
        out_specs=(
            P("seq", "head"),
            P("seq", "head"),
            P("seq", "head"),
            P("seq", "head"),
            P("seq", "head"),
        ),
        check_vma=False,
    )
```

```python
import math

import jax
import jax.numpy as jnp
from jax import lax
from jax.sharding import PartitionSpec as P

DH = 128
BLK = 128


LOG_TWO = math.log(2.0)


def swapped(value, axis, bit):
    mask = 2**bit
    pairs = [(source, source ^ mask) for source in range(lax.axis_size(axis))]
    return lax.ppermute(value, axis, pairs)


def pair_mean(tensor):
    shape_in = tensor.shape
    paired = tensor.reshape(shape_in[:-2] + (shape_in[-2] // 2, 2, shape_in[-1]))
    return jnp.sum(paired, axis=-2) * 0.5


def spread_rows(grads, factor):
    shape_in = grads.shape
    wide = jnp.broadcast_to(grads[..., :, None, :], shape_in[:-1] + (factor, shape_in[-1])) * (
        1.0 / factor
    )
    return wide.reshape(shape_in[:-2] + (shape_in[-2] * factor, shape_in[-1]))


def head_ring_gather(value, relative=False):
    count = lax.axis_size("head")
    rings = count // 2
    width = value.shape[-1]
    where_head = lax.axis_index("head")
    ring_pos = where_head // 2
    partner = lax.ppermute(value, "head", [(src, src ^ 1) for src in range(count)])
    low_first = where_head % 2 == 0
    pair_block = jnp.concatenate(
        [jnp.where(low_first, value, partner), jnp.where(low_first, partner, value)], axis=-1
    )
    upward = [(src, ((src // 2 + 1) % rings) * 2 + src % 2) for src in range(count)]
    downward = [(src, ((src // 2 - 1) % rings) * 2 + src % 2) for src in range(count)]
    from_below = lax.ppermute(pair_block, "head", upward)
    from_above = lax.ppermute(pair_block, "head", downward)
    blocks = [pair_block, from_above]
    if rings == 4:
        far = jnp.concatenate(
            [
                lax.ppermute(from_below[..., :width], "head", upward),
                lax.ppermute(from_above[..., width:], "head", downward),
            ],
            axis=-1,
        )
        blocks = [pair_block, from_above, far, from_below]
    if relative:
        return blocks
    stacked = jnp.stack(blocks)
    order = (jnp.arange(rings) - ring_pos) % rings
    placed = stacked[order]
    return jnp.moveaxis(placed, 0, -2).reshape(value.shape[:-1] + (rings * 2 * width,))


def weight_columns(out_weight):
    count = lax.axis_size("head")
    seq_count = lax.axis_size("seq")
    where_head = lax.axis_index("head")
    core = lax.axis_index("seq") % 2
    rows, cols = out_weight.shape
    width = cols // count
    own = lax.dynamic_slice_in_dim(out_weight, where_head * width, width, axis=1)
    fetched = []
    for step in range(count // 2):
        shift_low, shift_high = 2 * step + 1, 2 * step + 2
        pairs = []
        for seq_idx in range(seq_count):
            shift = shift_low if seq_idx % 2 == 0 else shift_high
            if shift % count == 0:
                continue
            for src in range(count):
                pairs.append((seq_idx * count + src, seq_idx * count + (src + shift) % count))
        shift = jnp.where(core == 0, shift_low, shift_high)
        outgoing = lax.dynamic_slice_in_dim(
            out_weight, ((where_head + shift) % count) * width, width, axis=1
        )
        fetched.append(lax.ppermute(outgoing, ("seq", "head"), pairs))
    mine = jnp.stack(fetched)
    theirs = lax.ppermute(mine, "seq", [(src, src ^ 1) for src in range(seq_count)])
    odd = jnp.where(core == 0, mine, theirs)
    even = jnp.where(core == 0, theirs, mine)
    by_shift = [own]
    for shift in range(1, count):
        by_shift.append(odd[(shift - 1) // 2] if shift % 2 else even[shift // 2 - 1])
    low_first = where_head % 2 == 0
    ring_blocks = []
    for dist in range(count // 2):
        ring_blocks.append(
            jnp.where(
                low_first,
                jnp.concatenate(
                    [by_shift[(-2 * dist) % count], by_shift[(-1 - 2 * dist) % count]], axis=0
                ),
                jnp.concatenate(
                    [by_shift[(1 - 2 * dist) % count], by_shift[(-2 * dist) % count]], axis=0
                ),
            )
        )
    return ring_blocks

def body(queries, key_rows, value_rows, out_weight, cotangent, pattern):
    row_count, features = queries.shape
    blocks = row_count // BLK
    local_levels = blocks.bit_length() - 1
    seq_count = lax.axis_size("seq")
    cross_levels = seq_count.bit_length() - 1
    level_count = local_levels + cross_levels
    head_count = features // DH
    keys_all = (1 + level_count) * BLK
    score_scale = DH ** (-0.5)
    where_seq = lax.axis_index("seq")
    stacked = jnp.stack([key_rows, value_rows])
    coarse_base = (
        stacked.reshape(2, BLK, row_count // BLK, features).astype(jnp.float32).mean(axis=2)
    )
    siblings = []
    current = coarse_base
    for level_idx in range(cross_levels):
        received = swapped(current, "seq", level_idx)
        siblings.append(received)
        if level_idx + 1 < cross_levels:
            upper_half = jnp.right_shift(where_seq, level_idx) & 1 == 1
            joined = jnp.where(
                upper_half,
                jnp.concatenate([received, current], axis=1),
                jnp.concatenate([current, received], axis=1),
            )
            current = pair_mean(joined)
    segments = [stacked.reshape(2, blocks, BLK, features)]
    for level_idx in range(local_levels):
        factor = 2**level_idx
        group_count = blocks >> level_idx
        if level_idx == 0:
            pooled = stacked
        else:
            pooled = (
                stacked.reshape(2, row_count // factor, factor, features)
                .astype(jnp.float32)
                .mean(axis=2)
                .astype(jnp.bfloat16)
            )
        sibling = pooled.reshape(2, group_count // 2, 2, BLK, features)[:, :, ::-1].reshape(
            2, group_count, BLK, features
        )
        segments.append(
            jnp.broadcast_to(sibling[:, :, None], (2, group_count, factor, BLK, features)).reshape(
                2, blocks, BLK, features
            )
        )
    key_set = jnp.concatenate(segments, axis=2)
    far_set = jnp.concatenate(
        [siblings[level_idx].astype(jnp.bfloat16) for level_idx in range(cross_levels)], axis=1
    )
    near_keys = (1 + local_levels) * BLK
    far_keys = cross_levels * BLK
    key_bias = jnp.concatenate(
        [jnp.zeros((BLK,), jnp.float32)]
        + [jnp.full((BLK,), level_idx * LOG_TWO, jnp.float32) for level_idx in range(level_count)]
    )
    level_flags = pattern == 1
    kept_mask = jnp.concatenate(
        [
            jnp.ones((blocks, BLK), bool),
            jnp.broadcast_to(level_flags[:, :, None], (blocks, level_count, BLK)).reshape(
                blocks, level_count * BLK
            ),
        ],
        axis=1,
    )
    query_heads = queries.reshape(blocks, BLK, head_count, DH)
    key_heads = key_set[0].reshape(blocks, near_keys, head_count, DH)
    value_heads = key_set[1].reshape(blocks, near_keys, head_count, DH)
    far_key_heads = far_set[0].reshape(far_keys, head_count, DH)
    far_value_heads = far_set[1].reshape(far_keys, head_count, DH)
    scores = (
        jnp.concatenate(
            [
                jnp.einsum(
                    "bqhd,bkhd->bhqk", query_heads, key_heads, preferred_element_type=jnp.float32
                ),
                jnp.einsum(
                    "bqhd,khd->bhqk", query_heads, far_key_heads, preferred_element_type=jnp.float32
                ),
            ],
            axis=-1,
        )
        * score_scale
        + key_bias
    )
    scores = jnp.where(kept_mask[:, None, None, :], scores, -jnp.inf)
    row_max = jnp.max(scores, axis=-1, keepdims=True)
    weights_raw = jnp.exp(scores - row_max)
    attn_prob = weights_raw / jnp.sum(weights_raw, axis=-1, keepdims=True)
    prob_low = attn_prob.astype(jnp.bfloat16)
    near_prob, far_prob = prob_low[..., :near_keys], prob_low[..., near_keys:]
    mixed = jnp.einsum(
        "bhqk,bkhd->bqhd", near_prob, value_heads, preferred_element_type=jnp.float32
    ) + jnp.einsum("bhqk,khd->bqhd", far_prob, far_value_heads, preferred_element_type=jnp.float32)
    attended = mixed.astype(jnp.bfloat16).reshape(row_count, features)
    attended, weight_cols = lax.optimization_barrier((attended, weight_columns(out_weight)))
    half_rows = row_count // 2
    grads_full = jnp.concatenate(
        [
            lax.all_gather(cotangent[:half_rows], "head", axis=1, tiled=True),
            head_ring_gather(cotangent[half_rows:]),
        ],
        axis=0,
    )
    grad_attn = lax.dot_general(
        grads_full, out_weight, (((1,), (1,)), ((), ())), preferred_element_type=jnp.float32
    ).astype(jnp.bfloat16)
    late_attended, grad_attn = lax.optimization_barrier((attended, grad_attn))
    attended_blocks = head_ring_gather(late_attended, relative=True)
    grad_weight = lax.psum_scatter(
        lax.dot_general(
            grads_full, attended, (((0,), (0,)), ((), ())), preferred_element_type=jnp.float32
        ),
        "seq",
        scatter_dimension=0,
        tiled=True,
    )
    grad_heads = grad_attn.reshape(blocks, BLK, head_count, DH)
    grad_prob = jnp.concatenate(
        [
            jnp.einsum(
                "bqhd,bkhd->bhqk", grad_heads, value_heads, preferred_element_type=jnp.float32
            ),
            jnp.einsum(
                "bqhd,khd->bhqk", grad_heads, far_value_heads, preferred_element_type=jnp.float32
            ),
        ],
        axis=-1,
    )
    row_delta = jnp.sum(attn_prob * grad_prob, axis=-1, keepdims=True)
    grad_score = (attn_prob * (grad_prob - row_delta)).astype(jnp.bfloat16)
    near_score, far_score = grad_score[..., :near_keys], grad_score[..., near_keys:]
    grad_query = (
        (
            (
                jnp.einsum(
                    "bhqk,bkhd->bqhd", near_score, key_heads, preferred_element_type=jnp.float32
                )
                + jnp.einsum(
                    "bhqk,khd->bqhd", far_score, far_key_heads, preferred_element_type=jnp.float32
                )
            )
            * score_scale
        )
        .astype(jnp.bfloat16)
        .reshape(row_count, features)
    )
    grad_keyset = (
        jnp.einsum("bhqk,bqhd->bkhd", near_score, query_heads, preferred_element_type=jnp.float32)
        * score_scale
    )
    grad_valset = jnp.einsum(
        "bhqk,bqhd->bkhd", near_prob, grad_heads, preferred_element_type=jnp.float32
    )
    grad_sets = jnp.stack([grad_keyset, grad_valset]).reshape(2, blocks, near_keys, features)
    far_grad_keys = (
        jnp.einsum("bhqk,bqhd->khd", far_score, query_heads, preferred_element_type=jnp.float32)
        * score_scale
    )
    far_grad_values = jnp.einsum(
        "bhqk,bqhd->khd", far_prob, grad_heads, preferred_element_type=jnp.float32
    )
    far_grads = jnp.stack([far_grad_keys, far_grad_values]).reshape(2, far_keys, features)
    token_grad = grad_sets[:, :, :BLK].reshape(2, row_count, features)
    level_grads = []
    for level_idx in range(local_levels):
        factor = 2**level_idx
        group_count = blocks >> level_idx
        lower = (level_idx + 1) * BLK
        segment = (
            grad_sets[:, :, lower : lower + BLK]
            .reshape(2, group_count, factor, BLK, features)
            .sum(axis=2)
        )
        restored = segment.reshape(2, group_count // 2, 2, BLK, features)[:, :, ::-1].reshape(
            2, group_count * BLK, features
        )
        level_grads.append(restored)
    sibling_grads = []
    for level_idx in range(cross_levels):
        sibling_grads.append(far_grads[:, level_idx * BLK : (level_idx + 1) * BLK])
    carried = jnp.zeros((2, BLK, features), jnp.float32)
    for level_idx in reversed(range(cross_levels)):
        outgoing = sibling_grads[level_idx]
        if level_idx + 1 < cross_levels:
            halves = spread_rows(carried, 2)
            lower_part = halves[:, :BLK]
            upper_part = halves[:, BLK:]
            upper_half = jnp.right_shift(where_seq, level_idx) & 1 == 1
            own_part = jnp.where(upper_half, upper_part, lower_part)
            outgoing = outgoing + jnp.where(upper_half, lower_part, upper_part)
        else:
            own_part = jnp.zeros_like(outgoing)
        carried = own_part + swapped(outgoing, "seq", level_idx)
    attended_blocks, carried = lax.optimization_barrier((attended_blocks, carried))
    output_sum = jnp.dot(attended_blocks[0], weight_cols[0], preferred_element_type=jnp.float32)
    for dist in range(1, len(attended_blocks)):
        output_sum = output_sum + jnp.dot(
            attended_blocks[dist], weight_cols[dist], preferred_element_type=jnp.float32
        )
    output = output_sum.astype(jnp.bfloat16)
    if local_levels:
        pooled_grad = level_grads[-1]
        for level_idx in reversed(range(local_levels - 1)):
            pooled_grad = level_grads[level_idx] + spread_rows(pooled_grad, 2)
        token_grad = token_grad + pooled_grad
    token_grad = token_grad + spread_rows(carried, 2**local_levels)
    grad_keys = token_grad[0].astype(jnp.bfloat16)
    grad_values = token_grad[1].astype(jnp.bfloat16)
    return (output, grad_query, grad_keys, grad_values, grad_weight)


def solution(mesh):
    placed = (
        P("seq", "head"),
        P("seq", "head"),
        P("seq", "head"),
        P("head", None),
        P("seq", "head"),
        P("seq", None),
    )
    return jax.shard_map(
        body,
        mesh=mesh,
        in_specs=placed,
        out_specs=(
            P("seq", "head"),
            P("seq", "head"),
            P("seq", "head"),
            P("seq", "head"),
            P("seq", "head"),
        ),
        check_vma=False,
    )
```

```python
import math

import jax
import jax.numpy as jnp
from jax import lax
from jax.sharding import PartitionSpec as P

DH = 128
BLK = 128


LOG_TWO = math.log(2.0)


def swapped(value, axis, bit):
    mask = 2**bit
    pairs = [(source, source ^ mask) for source in range(lax.axis_size(axis))]
    return lax.ppermute(value, axis, pairs)


def pair_mean(tensor):
    shape_in = tensor.shape
    paired = tensor.reshape(shape_in[:-2] + (shape_in[-2] // 2, 2, shape_in[-1]))
    return jnp.sum(paired, axis=-2) * 0.5


def spread_rows(grads, factor):
    shape_in = grads.shape
    wide = jnp.broadcast_to(grads[..., :, None, :], shape_in[:-1] + (factor, shape_in[-1])) * (
        1.0 / factor
    )
    return wide.reshape(shape_in[:-2] + (shape_in[-2] * factor, shape_in[-1]))


def head_ring_gather(value, relative=False):
    count = lax.axis_size("head")
    rings = count // 2
    width = value.shape[-1]
    where_head = lax.axis_index("head")
    ring_pos = where_head // 2
    partner = lax.ppermute(value, "head", [(src, src ^ 1) for src in range(count)])
    low_first = where_head % 2 == 0
    pair_block = jnp.concatenate(
        [jnp.where(low_first, value, partner), jnp.where(low_first, partner, value)], axis=-1
    )
    upward = [(src, ((src // 2 + 1) % rings) * 2 + src % 2) for src in range(count)]
    downward = [(src, ((src // 2 - 1) % rings) * 2 + src % 2) for src in range(count)]
    from_below = lax.ppermute(pair_block, "head", upward)
    from_above = lax.ppermute(pair_block, "head", downward)
    blocks = [pair_block, from_above]
    if rings == 4:
        far = jnp.concatenate(
            [
                lax.ppermute(from_below[..., :width], "head", upward),
                lax.ppermute(from_above[..., width:], "head", downward),
            ],
            axis=-1,
        )
        blocks = [pair_block, from_above, far, from_below]
    if relative:
        return blocks
    stacked = jnp.stack(blocks)
    order = (jnp.arange(rings) - ring_pos) % rings
    placed = stacked[order]
    return jnp.moveaxis(placed, 0, -2).reshape(value.shape[:-1] + (rings * 2 * width,))


def weight_columns(out_weight):
    count = lax.axis_size("head")
    seq_count = lax.axis_size("seq")
    where_head = lax.axis_index("head")
    core = lax.axis_index("seq") % 2
    rows, cols = out_weight.shape
    width = cols // count
    own = lax.dynamic_slice_in_dim(out_weight, where_head * width, width, axis=1)
    fetched = []
    for step in range(count // 2):
        shift_low, shift_high = 2 * step + 1, 2 * step + 2
        pairs = []
        for seq_idx in range(seq_count):
            shift = shift_low if seq_idx % 2 == 0 else shift_high
            if shift % count == 0:
                continue
            for src in range(count):
                pairs.append((seq_idx * count + src, seq_idx * count + (src + shift) % count))
        shift = jnp.where(core == 0, shift_low, shift_high)
        outgoing = lax.dynamic_slice_in_dim(
            out_weight, ((where_head + shift) % count) * width, width, axis=1
        )
        fetched.append(lax.ppermute(outgoing, ("seq", "head"), pairs))
    mine = jnp.stack(fetched)
    theirs = lax.ppermute(mine, "seq", [(src, src ^ 1) for src in range(seq_count)])
    odd = jnp.where(core == 0, mine, theirs)
    even = jnp.where(core == 0, theirs, mine)
    by_shift = [own]
    for shift in range(1, count):
        by_shift.append(odd[(shift - 1) // 2] if shift % 2 else even[shift // 2 - 1])
    low_first = where_head % 2 == 0
    ring_blocks = []
    for dist in range(count // 2):
        ring_blocks.append(
            jnp.where(
                low_first,
                jnp.concatenate(
                    [by_shift[(-2 * dist) % count], by_shift[(-1 - 2 * dist) % count]], axis=0
                ),
                jnp.concatenate(
                    [by_shift[(1 - 2 * dist) % count], by_shift[(-2 * dist) % count]], axis=0
                ),
            )
        )
    return ring_blocks

def body(queries, key_rows, value_rows, out_weight, cotangent, pattern):
    row_count, features = queries.shape
    blocks = row_count // BLK
    local_levels = blocks.bit_length() - 1
    seq_count = lax.axis_size("seq")
    cross_levels = seq_count.bit_length() - 1
    level_count = local_levels + cross_levels
    head_count = features // DH
    keys_all = (1 + level_count) * BLK
    score_scale = DH ** (-0.5)
    where_seq = lax.axis_index("seq")
    stacked = jnp.stack([key_rows, value_rows])
    coarse_base = (
        stacked.reshape(2, BLK, row_count // BLK, features).astype(jnp.float32).mean(axis=2)
    )
    siblings = []
    current = coarse_base
    for level_idx in range(cross_levels):
        received = swapped(current, "seq", level_idx)
        siblings.append(received)
        if level_idx + 1 < cross_levels:
            upper_half = jnp.right_shift(where_seq, level_idx) & 1 == 1
            joined = jnp.where(
                upper_half,
                jnp.concatenate([received, current], axis=1),
                jnp.concatenate([current, received], axis=1),
            )
            current = pair_mean(joined)
    segments = [stacked.reshape(2, blocks, BLK, features)]
    for level_idx in range(local_levels):
        factor = 2**level_idx
        group_count = blocks >> level_idx
        if level_idx == 0:
            pooled = stacked
        else:
            pooled = (
                stacked.reshape(2, row_count // factor, factor, features)
                .astype(jnp.float32)
                .mean(axis=2)
                .astype(jnp.bfloat16)
            )
        paired = pooled.reshape(2, group_count // 2, 2, BLK, features)
        sibling = jnp.concatenate([paired[:, :, 1:], paired[:, :, :1]], axis=2).reshape(
            2, group_count, BLK, features
        )
        segments.append(
            jnp.broadcast_to(sibling[:, :, None], (2, group_count, factor, BLK, features)).reshape(
                2, blocks, BLK, features
            )
        )
    key_set = jnp.concatenate(segments, axis=2)
    far_set = jnp.concatenate(
        [siblings[level_idx].astype(jnp.bfloat16) for level_idx in range(cross_levels)], axis=1
    )
    near_keys = (1 + local_levels) * BLK
    far_keys = cross_levels * BLK
    key_bias = jnp.concatenate(
        [jnp.zeros((BLK,), jnp.float32)]
        + [jnp.full((BLK,), level_idx * LOG_TWO, jnp.float32) for level_idx in range(level_count)]
    )
    level_flags = pattern == 1
    kept_mask = jnp.concatenate(
        [
            jnp.ones((blocks, BLK), bool),
            jnp.broadcast_to(level_flags[:, :, None], (blocks, level_count, BLK)).reshape(
                blocks, level_count * BLK
            ),
        ],
        axis=1,
    )
    query_heads = queries.reshape(blocks, BLK, head_count, DH)
    key_heads = key_set[0].reshape(blocks, near_keys, head_count, DH)
    value_heads = key_set[1].reshape(blocks, near_keys, head_count, DH)
    far_key_heads = far_set[0].reshape(far_keys, head_count, DH)
    far_value_heads = far_set[1].reshape(far_keys, head_count, DH)
    scores = (
        jnp.concatenate(
            [
                jnp.einsum(
                    "bqhd,bkhd->bhqk", query_heads, key_heads, preferred_element_type=jnp.float32
                ),
                jnp.einsum(
                    "bqhd,khd->bhqk", query_heads, far_key_heads, preferred_element_type=jnp.float32
                ),
            ],
            axis=-1,
        )
        * score_scale
        + key_bias
    )
    scores = jnp.where(kept_mask[:, None, None, :], scores, -jnp.inf)
    row_max = jnp.max(scores, axis=-1, keepdims=True)
    weights_raw = jnp.exp(scores - row_max)
    attn_prob = weights_raw / jnp.sum(weights_raw, axis=-1, keepdims=True)
    prob_low = attn_prob.astype(jnp.bfloat16)
    near_prob, far_prob = prob_low[..., :near_keys], prob_low[..., near_keys:]
    mixed = jnp.einsum(
        "bhqk,bkhd->bqhd", near_prob, value_heads, preferred_element_type=jnp.float32
    ) + jnp.einsum("bhqk,khd->bqhd", far_prob, far_value_heads, preferred_element_type=jnp.float32)
    attended = mixed.astype(jnp.bfloat16).reshape(row_count, features)
    attended, weight_cols = lax.optimization_barrier((attended, weight_columns(out_weight)))
    half_rows = row_count // 2
    grads_full = jnp.concatenate(
        [
            lax.all_gather(cotangent[:half_rows], "head", axis=1, tiled=True),
            head_ring_gather(cotangent[half_rows:]),
        ],
        axis=0,
    )
    grad_attn = lax.dot_general(
        grads_full, out_weight, (((1,), (1,)), ((), ())), preferred_element_type=jnp.float32
    ).astype(jnp.bfloat16)
    late_attended, grad_attn = lax.optimization_barrier((attended, grad_attn))
    attended_blocks = head_ring_gather(late_attended, relative=True)
    grad_weight = lax.psum_scatter(
        lax.dot_general(
            grads_full, attended, (((0,), (0,)), ((), ())), preferred_element_type=jnp.float32
        ),
        "seq",
        scatter_dimension=0,
        tiled=True,
    )
    grad_heads = grad_attn.reshape(blocks, BLK, head_count, DH)
    grad_prob = jnp.concatenate(
        [
            jnp.einsum(
                "bqhd,bkhd->bhqk", grad_heads, value_heads, preferred_element_type=jnp.float32
            ),
            jnp.einsum(
                "bqhd,khd->bhqk", grad_heads, far_value_heads, preferred_element_type=jnp.float32
            ),
        ],
        axis=-1,
    )
    row_delta = jnp.sum(attn_prob * grad_prob, axis=-1, keepdims=True)
    grad_score = (attn_prob * (grad_prob - row_delta)).astype(jnp.bfloat16)
    near_score, far_score = grad_score[..., :near_keys], grad_score[..., near_keys:]
    grad_query = (
        (
            (
                jnp.einsum(
                    "bhqk,bkhd->bqhd", near_score, key_heads, preferred_element_type=jnp.float32
                )
                + jnp.einsum(
                    "bhqk,khd->bqhd", far_score, far_key_heads, preferred_element_type=jnp.float32
                )
            )
            * score_scale
        )
        .astype(jnp.bfloat16)
        .reshape(row_count, features)
    )
    grad_keyset = (
        jnp.einsum("bhqk,bqhd->bkhd", near_score, query_heads, preferred_element_type=jnp.float32)
        * score_scale
    )
    grad_valset = jnp.einsum(
        "bhqk,bqhd->bkhd", near_prob, grad_heads, preferred_element_type=jnp.float32
    )
    grad_sets = jnp.stack([grad_keyset, grad_valset]).reshape(2, blocks, near_keys, features)
    far_grad_keys = (
        jnp.einsum("bhqk,bqhd->khd", far_score, query_heads, preferred_element_type=jnp.float32)
        * score_scale
    )
    far_grad_values = jnp.einsum(
        "bhqk,bqhd->khd", far_prob, grad_heads, preferred_element_type=jnp.float32
    )
    far_grads = jnp.stack([far_grad_keys, far_grad_values]).reshape(2, far_keys, features)
    token_grad = grad_sets[:, :, :BLK].reshape(2, row_count, features)
    level_grads = []
    for level_idx in range(local_levels):
        factor = 2**level_idx
        group_count = blocks >> level_idx
        lower = (level_idx + 1) * BLK
        segment = (
            grad_sets[:, :, lower : lower + BLK]
            .reshape(2, group_count, factor, BLK, features)
            .sum(axis=2)
        )
        paired = segment.reshape(2, group_count // 2, 2, BLK, features)
        restored = jnp.concatenate([paired[:, :, 1:], paired[:, :, :1]], axis=2).reshape(
            2, group_count * BLK, features
        )
        level_grads.append(restored)
    sibling_grads = []
    for level_idx in range(cross_levels):
        sibling_grads.append(far_grads[:, level_idx * BLK : (level_idx + 1) * BLK])
    carried = jnp.zeros((2, BLK, features), jnp.float32)
    for level_idx in reversed(range(cross_levels)):
        outgoing = sibling_grads[level_idx]
        if level_idx + 1 < cross_levels:
            halves = spread_rows(carried, 2)
            lower_part = halves[:, :BLK]
            upper_part = halves[:, BLK:]
            upper_half = jnp.right_shift(where_seq, level_idx) & 1 == 1
            own_part = jnp.where(upper_half, upper_part, lower_part)
            outgoing = outgoing + jnp.where(upper_half, lower_part, upper_part)
        else:
            own_part = jnp.zeros_like(outgoing)
        carried = own_part + swapped(outgoing, "seq", level_idx)
    attended_blocks, carried = lax.optimization_barrier((attended_blocks, carried))
    output_sum = jnp.dot(attended_blocks[0], weight_cols[0], preferred_element_type=jnp.float32)
    for dist in range(1, len(attended_blocks)):
        output_sum = output_sum + jnp.dot(
            attended_blocks[dist], weight_cols[dist], preferred_element_type=jnp.float32
        )
    output = output_sum.astype(jnp.bfloat16)
    if local_levels:
        pooled_grad = level_grads[-1]
        for level_idx in reversed(range(local_levels - 1)):
            pooled_grad = level_grads[level_idx] + spread_rows(pooled_grad, 2)
        token_grad = token_grad + pooled_grad
    token_grad = token_grad + spread_rows(carried, 2**local_levels)
    grad_keys = token_grad[0].astype(jnp.bfloat16)
    grad_values = token_grad[1].astype(jnp.bfloat16)
    return (output, grad_query, grad_keys, grad_values, grad_weight)


def solution(mesh):
    placed = (
        P("seq", "head"),
        P("seq", "head"),
        P("seq", "head"),
        P("head", None),
        P("seq", "head"),
        P("seq", None),
    )
    return jax.shard_map(
        body,
        mesh=mesh,
        in_specs=placed,
        out_specs=(
            P("seq", "head"),
            P("seq", "head"),
            P("seq", "head"),
            P("seq", "head"),
            P("seq", "head"),
        ),
        check_vma=False,
    )
```

```python
import math

import jax
import jax.numpy as jnp
from jax import lax
from jax.sharding import PartitionSpec as P

DH = 128
BLK = 128


LOG_TWO = math.log(2.0)


def swapped(value, axis, bit):
    mask = 2**bit
    pairs = [(source, source ^ mask) for source in range(lax.axis_size(axis))]
    return lax.ppermute(value, axis, pairs)


def pair_mean(tensor):
    shape_in = tensor.shape
    paired = tensor.reshape(shape_in[:-2] + (shape_in[-2] // 2, 2, shape_in[-1]))
    return jnp.sum(paired, axis=-2) * 0.5


def spread_rows(grads, factor):
    shape_in = grads.shape
    wide = jnp.broadcast_to(grads[..., :, None, :], shape_in[:-1] + (factor, shape_in[-1])) * (
        1.0 / factor
    )
    return wide.reshape(shape_in[:-2] + (shape_in[-2] * factor, shape_in[-1]))


def head_ring_gather(value, relative=False):
    count = lax.axis_size("head")
    rings = count // 2
    width = value.shape[-1]
    where_head = lax.axis_index("head")
    ring_pos = where_head // 2
    partner = lax.ppermute(value, "head", [(src, src ^ 1) for src in range(count)])
    low_first = where_head % 2 == 0
    pair_block = jnp.concatenate(
        [jnp.where(low_first, value, partner), jnp.where(low_first, partner, value)], axis=-1
    )
    upward = [(src, ((src // 2 + 1) % rings) * 2 + src % 2) for src in range(count)]
    downward = [(src, ((src // 2 - 1) % rings) * 2 + src % 2) for src in range(count)]
    from_below = lax.ppermute(pair_block, "head", upward)
    from_above = lax.ppermute(pair_block, "head", downward)
    blocks = [pair_block, from_above]
    if rings == 4:
        far = jnp.concatenate(
            [
                lax.ppermute(from_below[..., :width], "head", upward),
                lax.ppermute(from_above[..., width:], "head", downward),
            ],
            axis=-1,
        )
        blocks = [pair_block, from_above, far, from_below]
    if relative:
        return blocks
    stacked = jnp.stack(blocks)
    order = (jnp.arange(rings) - ring_pos) % rings
    placed = stacked[order]
    return jnp.moveaxis(placed, 0, -2).reshape(value.shape[:-1] + (rings * 2 * width,))


def weight_columns(out_weight):
    count = lax.axis_size("head")
    seq_count = lax.axis_size("seq")
    where_head = lax.axis_index("head")
    core = lax.axis_index("seq") % 2
    rows, cols = out_weight.shape
    width = cols // count
    own = lax.dynamic_slice_in_dim(out_weight, where_head * width, width, axis=1)
    fetched = []
    for step in range(count // 2):
        shift_low, shift_high = 2 * step + 1, 2 * step + 2
        pairs = []
        for seq_idx in range(seq_count):
            shift = shift_low if seq_idx % 2 == 0 else shift_high
            if shift % count == 0:
                continue
            for src in range(count):
                pairs.append((seq_idx * count + src, seq_idx * count + (src + shift) % count))
        shift = jnp.where(core == 0, shift_low, shift_high)
        outgoing = lax.dynamic_slice_in_dim(
            out_weight, ((where_head + shift) % count) * width, width, axis=1
        )
        fetched.append(lax.ppermute(outgoing, ("seq", "head"), pairs))
    mine = jnp.stack(fetched)
    theirs = lax.ppermute(mine, "seq", [(src, src ^ 1) for src in range(seq_count)])
    odd = jnp.where(core == 0, mine, theirs)
    even = jnp.where(core == 0, theirs, mine)
    by_shift = [own]
    for shift in range(1, count):
        by_shift.append(odd[(shift - 1) // 2] if shift % 2 else even[shift // 2 - 1])
    low_first = where_head % 2 == 0
    ring_blocks = []
    for dist in range(count // 2):
        ring_blocks.append(
            jnp.where(
                low_first,
                jnp.concatenate(
                    [by_shift[(-2 * dist) % count], by_shift[(-1 - 2 * dist) % count]], axis=0
                ),
                jnp.concatenate(
                    [by_shift[(1 - 2 * dist) % count], by_shift[(-2 * dist) % count]], axis=0
                ),
            )
        )
    return ring_blocks

def body(queries, key_rows, value_rows, out_weight, cotangent, pattern):
    row_count, features = queries.shape
    blocks = row_count // BLK
    local_levels = blocks.bit_length() - 1
    seq_count = lax.axis_size("seq")
    cross_levels = seq_count.bit_length() - 1
    level_count = local_levels + cross_levels
    head_count = features // DH
    keys_all = (1 + level_count) * BLK
    score_scale = DH ** (-0.5)
    where_seq = lax.axis_index("seq")
    stacked = jnp.stack([key_rows, value_rows])
    coarse_base = (
        stacked.reshape(2, BLK, row_count // BLK, features).astype(jnp.float32).mean(axis=2)
    )
    siblings = []
    current = coarse_base
    for level_idx in range(cross_levels):
        received = swapped(current, "seq", level_idx)
        siblings.append(received)
        if level_idx + 1 < cross_levels:
            upper_half = jnp.right_shift(where_seq, level_idx) & 1 == 1
            joined = jnp.where(
                upper_half,
                jnp.concatenate([received, current], axis=1),
                jnp.concatenate([current, received], axis=1),
            )
            current = pair_mean(joined)
    segments = [stacked.reshape(2, blocks, BLK, features)]
    for level_idx in range(local_levels):
        factor = 2**level_idx
        group_count = blocks >> level_idx
        if level_idx == 0:
            pooled = stacked
        else:
            pooled = (
                stacked.reshape(2, row_count // factor, factor, features)
                .astype(jnp.float32)
                .mean(axis=2)
                .astype(jnp.bfloat16)
            )
        paired = pooled.reshape(2, group_count // 2, 2, BLK, features)
        sibling = jnp.concatenate([paired[:, :, 1:], paired[:, :, :1]], axis=2).reshape(
            2, group_count, BLK, features
        )
        segments.append(
            jnp.broadcast_to(sibling[:, :, None], (2, group_count, factor, BLK, features)).reshape(
                2, blocks, BLK, features
            )
        )
    key_set = jnp.concatenate(segments, axis=2)
    far_set = jnp.concatenate(
        [siblings[level_idx].astype(jnp.bfloat16) for level_idx in range(cross_levels)], axis=1
    )
    near_keys = (1 + local_levels) * BLK
    far_keys = cross_levels * BLK
    key_bias = jnp.concatenate(
        [jnp.zeros((BLK,), jnp.float32)]
        + [jnp.full((BLK,), level_idx * LOG_TWO, jnp.float32) for level_idx in range(level_count)]
    )
    level_flags = pattern == 1
    kept_mask = jnp.concatenate(
        [
            jnp.ones((blocks, BLK), bool),
            jnp.broadcast_to(level_flags[:, :, None], (blocks, level_count, BLK)).reshape(
                blocks, level_count * BLK
            ),
        ],
        axis=1,
    )
    query_heads = queries.reshape(blocks, BLK, head_count, DH)
    key_heads = key_set[0].reshape(blocks, near_keys, head_count, DH)
    value_heads = key_set[1].reshape(blocks, near_keys, head_count, DH)
    far_key_heads = far_set[0].reshape(far_keys, head_count, DH)
    far_value_heads = far_set[1].reshape(far_keys, head_count, DH)
    scores = (
        jnp.concatenate(
            [
                jnp.einsum(
                    "bqhd,bkhd->bhqk", query_heads, key_heads, preferred_element_type=jnp.float32
                ),
                jnp.einsum(
                    "bqhd,khd->bhqk", query_heads, far_key_heads, preferred_element_type=jnp.float32
                ),
            ],
            axis=-1,
        )
        * score_scale
        + key_bias
    )
    scores = jnp.where(kept_mask[:, None, None, :], scores, -jnp.inf)
    row_max = jnp.max(scores, axis=-1, keepdims=True)
    weights_raw = jnp.exp(scores - row_max)
    attn_prob = weights_raw / jnp.sum(weights_raw, axis=-1, keepdims=True)
    prob_low = attn_prob.astype(jnp.bfloat16)
    near_prob, far_prob = prob_low[..., :near_keys], prob_low[..., near_keys:]
    mixed = jnp.einsum(
        "bhqk,bkhd->bqhd", near_prob, value_heads, preferred_element_type=jnp.float32
    ) + jnp.einsum("bhqk,khd->bqhd", far_prob, far_value_heads, preferred_element_type=jnp.float32)
    attended = mixed.astype(jnp.bfloat16).reshape(row_count, features)
    attended, weight_cols = lax.optimization_barrier((attended, weight_columns(out_weight)))
    half_rows = row_count // 4
    grads_full = jnp.concatenate(
        [
            lax.all_gather(cotangent[:half_rows], "head", axis=1, tiled=True),
            head_ring_gather(cotangent[half_rows:]),
        ],
        axis=0,
    )
    grad_attn = lax.dot_general(
        grads_full, out_weight, (((1,), (1,)), ((), ())), preferred_element_type=jnp.float32
    ).astype(jnp.bfloat16)
    late_attended, grad_attn = lax.optimization_barrier((attended, grad_attn))
    attended_blocks = head_ring_gather(late_attended, relative=True)
    grad_weight = lax.psum_scatter(
        lax.dot_general(
            grads_full, attended, (((0,), (0,)), ((), ())), preferred_element_type=jnp.float32
        ),
        "seq",
        scatter_dimension=0,
        tiled=True,
    )
    grad_heads = grad_attn.reshape(blocks, BLK, head_count, DH)
    grad_prob = jnp.concatenate(
        [
            jnp.einsum(
                "bqhd,bkhd->bhqk", grad_heads, value_heads, preferred_element_type=jnp.float32
            ),
            jnp.einsum(
                "bqhd,khd->bhqk", grad_heads, far_value_heads, preferred_element_type=jnp.float32
            ),
        ],
        axis=-1,
    )
    row_delta = jnp.sum(attn_prob * grad_prob, axis=-1, keepdims=True)
    grad_score = (attn_prob * (grad_prob - row_delta)).astype(jnp.bfloat16)
    near_score, far_score = grad_score[..., :near_keys], grad_score[..., near_keys:]
    grad_query = (
        (
            (
                jnp.einsum(
                    "bhqk,bkhd->bqhd", near_score, key_heads, preferred_element_type=jnp.float32
                )
                + jnp.einsum(
                    "bhqk,khd->bqhd", far_score, far_key_heads, preferred_element_type=jnp.float32
                )
            )
            * score_scale
        )
        .astype(jnp.bfloat16)
        .reshape(row_count, features)
    )
    grad_keyset = (
        jnp.einsum("bhqk,bqhd->bkhd", near_score, query_heads, preferred_element_type=jnp.float32)
        * score_scale
    )
    grad_valset = jnp.einsum(
        "bhqk,bqhd->bkhd", near_prob, grad_heads, preferred_element_type=jnp.float32
    )
    grad_sets = jnp.stack([grad_keyset, grad_valset]).reshape(2, blocks, near_keys, features)
    far_grad_keys = (
        jnp.einsum("bhqk,bqhd->khd", far_score, query_heads, preferred_element_type=jnp.float32)
        * score_scale
    )
    far_grad_values = jnp.einsum(
        "bhqk,bqhd->khd", far_prob, grad_heads, preferred_element_type=jnp.float32
    )
    far_grads = jnp.stack([far_grad_keys, far_grad_values]).reshape(2, far_keys, features)
    token_grad = grad_sets[:, :, :BLK].reshape(2, row_count, features)
    level_grads = []
    for level_idx in range(local_levels):
        factor = 2**level_idx
        group_count = blocks >> level_idx
        lower = (level_idx + 1) * BLK
        segment = (
            grad_sets[:, :, lower : lower + BLK]
            .reshape(2, group_count, factor, BLK, features)
            .sum(axis=2)
        )
        paired = segment.reshape(2, group_count // 2, 2, BLK, features)
        restored = jnp.concatenate([paired[:, :, 1:], paired[:, :, :1]], axis=2).reshape(
            2, group_count * BLK, features
        )
        level_grads.append(restored)
    sibling_grads = []
    for level_idx in range(cross_levels):
        sibling_grads.append(far_grads[:, level_idx * BLK : (level_idx + 1) * BLK])
    carried = jnp.zeros((2, BLK, features), jnp.float32)
    for level_idx in reversed(range(cross_levels)):
        outgoing = sibling_grads[level_idx]
        if level_idx + 1 < cross_levels:
            halves = spread_rows(carried, 2)
            lower_part = halves[:, :BLK]
            upper_part = halves[:, BLK:]
            upper_half = jnp.right_shift(where_seq, level_idx) & 1 == 1
            own_part = jnp.where(upper_half, upper_part, lower_part)
            outgoing = outgoing + jnp.where(upper_half, lower_part, upper_part)
        else:
            own_part = jnp.zeros_like(outgoing)
        carried = own_part + swapped(outgoing, "seq", level_idx)
    attended_blocks, carried = lax.optimization_barrier((attended_blocks, carried))
    output_sum = jnp.dot(attended_blocks[0], weight_cols[0], preferred_element_type=jnp.float32)
    for dist in range(1, len(attended_blocks)):
        output_sum = output_sum + jnp.dot(
            attended_blocks[dist], weight_cols[dist], preferred_element_type=jnp.float32
        )
    output = output_sum.astype(jnp.bfloat16)
    if local_levels:
        pooled_grad = level_grads[-1]
        for level_idx in reversed(range(local_levels - 1)):
            pooled_grad = level_grads[level_idx] + spread_rows(pooled_grad, 2)
        token_grad = token_grad + pooled_grad
    token_grad = token_grad + spread_rows(carried, 2**local_levels)
    grad_keys = token_grad[0].astype(jnp.bfloat16)
    grad_values = token_grad[1].astype(jnp.bfloat16)
    return (output, grad_query, grad_keys, grad_values, grad_weight)


def solution(mesh):
    placed = (
        P("seq", "head"),
        P("seq", "head"),
        P("seq", "head"),
        P("head", None),
        P("seq", "head"),
        P("seq", None),
    )
    return jax.shard_map(
        body,
        mesh=mesh,
        in_specs=placed,
        out_specs=(
            P("seq", "head"),
            P("seq", "head"),
            P("seq", "head"),
            P("seq", "head"),
            P("seq", "head"),
        ),
        check_vma=False,
    )
```

```python
import math

import jax
import jax.numpy as jnp
from jax import lax
from jax.sharding import PartitionSpec as P

DH = 128
BLK = 128


LOG_TWO = math.log(2.0)


def swapped(value, axis, bit):
    mask = 2**bit
    pairs = [(source, source ^ mask) for source in range(lax.axis_size(axis))]
    return lax.ppermute(value, axis, pairs)


def pair_mean(tensor):
    shape_in = tensor.shape
    paired = tensor.reshape(shape_in[:-2] + (shape_in[-2] // 2, 2, shape_in[-1]))
    return jnp.sum(paired, axis=-2) * 0.5


def spread_rows(grads, factor):
    shape_in = grads.shape
    wide = jnp.broadcast_to(grads[..., :, None, :], shape_in[:-1] + (factor, shape_in[-1])) * (
        1.0 / factor
    )
    return wide.reshape(shape_in[:-2] + (shape_in[-2] * factor, shape_in[-1]))


def head_ring_gather(value, relative=False):
    count = lax.axis_size("head")
    rings = count // 2
    width = value.shape[-1]
    where_head = lax.axis_index("head")
    ring_pos = where_head // 2
    partner = lax.ppermute(value, "head", [(src, src ^ 1) for src in range(count)])
    low_first = where_head % 2 == 0
    if relative:
        pair_block = jnp.concatenate([value, partner], axis=-1)
    else:
        pair_block = jnp.concatenate(
            [jnp.where(low_first, value, partner), jnp.where(low_first, partner, value)], axis=-1
        )
    upward = [(src, ((src // 2 + 1) % rings) * 2 + src % 2) for src in range(count)]
    downward = [(src, ((src // 2 - 1) % rings) * 2 + src % 2) for src in range(count)]
    from_below = lax.ppermute(pair_block, "head", upward)
    from_above = lax.ppermute(pair_block, "head", downward)
    blocks = [pair_block, from_above]
    if rings == 4:
        far = jnp.concatenate(
            [
                lax.ppermute(from_below[..., :width], "head", upward),
                lax.ppermute(from_above[..., width:], "head", downward),
            ],
            axis=-1,
        )
        blocks = [pair_block, from_above, far, from_below]
    if relative:
        return blocks
    stacked = jnp.stack(blocks)
    order = (jnp.arange(rings) - ring_pos) % rings
    placed = stacked[order]
    return jnp.moveaxis(placed, 0, -2).reshape(value.shape[:-1] + (rings * 2 * width,))


def weight_columns(out_weight):
    count = lax.axis_size("head")
    seq_count = lax.axis_size("seq")
    where_head = lax.axis_index("head")
    core = lax.axis_index("seq") % 2
    rows, cols = out_weight.shape
    width = cols // count
    own = lax.dynamic_slice_in_dim(out_weight, where_head * width, width, axis=1)
    fetched = []
    for step in range(count // 2):
        shift_low, shift_high = 2 * step + 1, 2 * step + 2
        pairs = []
        for seq_idx in range(seq_count):
            shift = shift_low if seq_idx % 2 == 0 else shift_high
            if shift % count == 0:
                continue
            for src in range(count):
                pairs.append((seq_idx * count + src, seq_idx * count + (src + shift) % count))
        shift = jnp.where(core == 0, shift_low, shift_high)
        outgoing = lax.dynamic_slice_in_dim(
            out_weight, ((where_head + shift) % count) * width, width, axis=1
        )
        fetched.append(lax.ppermute(outgoing, ("seq", "head"), pairs))
    mine = jnp.stack(fetched)
    theirs = lax.ppermute(mine, "seq", [(src, src ^ 1) for src in range(seq_count)])
    odd = jnp.where(core == 0, mine, theirs)
    even = jnp.where(core == 0, theirs, mine)
    by_shift = [own]
    for shift in range(1, count):
        by_shift.append(odd[(shift - 1) // 2] if shift % 2 else even[shift // 2 - 1])
    low_first = where_head % 2 == 0
    ring_blocks = []
    for dist in range(count // 2):
        ring_blocks.append(
            jnp.concatenate(
                [
                    by_shift[(-2 * dist) % count],
                    jnp.where(
                        low_first,
                        by_shift[(-1 - 2 * dist) % count],
                        by_shift[(1 - 2 * dist) % count],
                    ),
                ],
                axis=0,
            )
        )
    return ring_blocks

def body(queries, key_rows, value_rows, out_weight, cotangent, pattern):
    row_count, features = queries.shape
    blocks = row_count // BLK
    local_levels = blocks.bit_length() - 1
    seq_count = lax.axis_size("seq")
    cross_levels = seq_count.bit_length() - 1
    level_count = local_levels + cross_levels
    head_count = features // DH
    keys_all = (1 + level_count) * BLK
    score_scale = DH ** (-0.5)
    where_seq = lax.axis_index("seq")
    stacked = jnp.stack([key_rows, value_rows])
    coarse_base = (
        stacked.reshape(2, BLK, row_count // BLK, features).astype(jnp.float32).mean(axis=2)
    )
    siblings = []
    current = coarse_base
    for level_idx in range(cross_levels):
        received = swapped(current, "seq", level_idx)
        siblings.append(received)
        if level_idx + 1 < cross_levels:
            upper_half = jnp.right_shift(where_seq, level_idx) & 1 == 1
            joined = jnp.where(
                upper_half,
                jnp.concatenate([received, current], axis=1),
                jnp.concatenate([current, received], axis=1),
            )
            current = pair_mean(joined)
    segments = [stacked.reshape(2, blocks, BLK, features)]
    for level_idx in range(local_levels):
        factor = 2**level_idx
        group_count = blocks >> level_idx
        if level_idx == 0:
            pooled = stacked
        else:
            pooled = (
                stacked.reshape(2, row_count // factor, factor, features)
                .astype(jnp.float32)
                .mean(axis=2)
                .astype(jnp.bfloat16)
            )
        paired = pooled.reshape(2, group_count // 2, 2, BLK, features)
        sibling = jnp.concatenate([paired[:, :, 1:], paired[:, :, :1]], axis=2).reshape(
            2, group_count, BLK, features
        )
        segments.append(
            jnp.broadcast_to(sibling[:, :, None], (2, group_count, factor, BLK, features)).reshape(
                2, blocks, BLK, features
            )
        )
    key_set = jnp.concatenate(segments, axis=2)
    far_set = jnp.concatenate(
        [siblings[level_idx].astype(jnp.bfloat16) for level_idx in range(cross_levels)], axis=1
    )
    near_keys = (1 + local_levels) * BLK
    far_keys = cross_levels * BLK
    key_bias = jnp.concatenate(
        [jnp.zeros((BLK,), jnp.float32)]
        + [jnp.full((BLK,), level_idx * LOG_TWO, jnp.float32) for level_idx in range(level_count)]
    )
    level_flags = pattern == 1
    kept_mask = jnp.concatenate(
        [
            jnp.ones((blocks, BLK), bool),
            jnp.broadcast_to(level_flags[:, :, None], (blocks, level_count, BLK)).reshape(
                blocks, level_count * BLK
            ),
        ],
        axis=1,
    )
    query_heads = queries.reshape(blocks, BLK, head_count, DH)
    key_heads = key_set[0].reshape(blocks, near_keys, head_count, DH)
    value_heads = key_set[1].reshape(blocks, near_keys, head_count, DH)
    far_key_heads = far_set[0].reshape(far_keys, head_count, DH)
    far_value_heads = far_set[1].reshape(far_keys, head_count, DH)
    scores = (
        jnp.concatenate(
            [
                jnp.einsum(
                    "bqhd,bkhd->bhqk", query_heads, key_heads, preferred_element_type=jnp.float32
                ),
                jnp.einsum(
                    "bqhd,khd->bhqk", query_heads, far_key_heads, preferred_element_type=jnp.float32
                ),
            ],
            axis=-1,
        )
        * score_scale
        + key_bias
    )
    scores = jnp.where(kept_mask[:, None, None, :], scores, -jnp.inf)
    row_max = jnp.max(scores, axis=-1, keepdims=True)
    weights_raw = jnp.exp(scores - row_max)
    attn_prob = weights_raw / jnp.sum(weights_raw, axis=-1, keepdims=True)
    prob_low = attn_prob.astype(jnp.bfloat16)
    near_prob, far_prob = prob_low[..., :near_keys], prob_low[..., near_keys:]
    mixed = jnp.einsum(
        "bhqk,bkhd->bqhd", near_prob, value_heads, preferred_element_type=jnp.float32
    ) + jnp.einsum("bhqk,khd->bqhd", far_prob, far_value_heads, preferred_element_type=jnp.float32)
    attended = mixed.astype(jnp.bfloat16).reshape(row_count, features)
    attended, weight_cols = lax.optimization_barrier((attended, weight_columns(out_weight)))
    half_rows = row_count // 2
    grads_full = jnp.concatenate(
        [
            lax.all_gather(cotangent[:half_rows], "head", axis=1, tiled=True),
            head_ring_gather(cotangent[half_rows:]),
        ],
        axis=0,
    )
    grad_attn = lax.dot_general(
        grads_full, out_weight, (((1,), (1,)), ((), ())), preferred_element_type=jnp.float32
    ).astype(jnp.bfloat16)
    late_attended, grad_attn = lax.optimization_barrier((attended, grad_attn))
    attended_blocks = head_ring_gather(late_attended, relative=True)
    grad_weight = lax.psum_scatter(
        lax.dot_general(
            grads_full, attended, (((0,), (0,)), ((), ())), preferred_element_type=jnp.float32
        ),
        "seq",
        scatter_dimension=0,
        tiled=True,
    )
    grad_heads = grad_attn.reshape(blocks, BLK, head_count, DH)
    grad_prob = jnp.concatenate(
        [
            jnp.einsum(
                "bqhd,bkhd->bhqk", grad_heads, value_heads, preferred_element_type=jnp.float32
            ),
            jnp.einsum(
                "bqhd,khd->bhqk", grad_heads, far_value_heads, preferred_element_type=jnp.float32
            ),
        ],
        axis=-1,
    )
    row_delta = jnp.sum(attn_prob * grad_prob, axis=-1, keepdims=True)
    grad_score = (attn_prob * (grad_prob - row_delta)).astype(jnp.bfloat16)
    near_score, far_score = grad_score[..., :near_keys], grad_score[..., near_keys:]
    grad_query = (
        (
            (
                jnp.einsum(
                    "bhqk,bkhd->bqhd", near_score, key_heads, preferred_element_type=jnp.float32
                )
                + jnp.einsum(
                    "bhqk,khd->bqhd", far_score, far_key_heads, preferred_element_type=jnp.float32
                )
            )
            * score_scale
        )
        .astype(jnp.bfloat16)
        .reshape(row_count, features)
    )
    grad_keyset = (
        jnp.einsum("bhqk,bqhd->bkhd", near_score, query_heads, preferred_element_type=jnp.float32)
        * score_scale
    )
    grad_valset = jnp.einsum(
        "bhqk,bqhd->bkhd", near_prob, grad_heads, preferred_element_type=jnp.float32
    )
    grad_sets = jnp.stack([grad_keyset, grad_valset]).reshape(2, blocks, near_keys, features)
    far_grad_keys = (
        jnp.einsum("bhqk,bqhd->khd", far_score, query_heads, preferred_element_type=jnp.float32)
        * score_scale
    )
    far_grad_values = jnp.einsum(
        "bhqk,bqhd->khd", far_prob, grad_heads, preferred_element_type=jnp.float32
    )
    far_grads = jnp.stack([far_grad_keys, far_grad_values]).reshape(2, far_keys, features)
    token_grad = grad_sets[:, :, :BLK].reshape(2, row_count, features)
    level_grads = []
    for level_idx in range(local_levels):
        factor = 2**level_idx
        group_count = blocks >> level_idx
        lower = (level_idx + 1) * BLK
        segment = (
            grad_sets[:, :, lower : lower + BLK]
            .reshape(2, group_count, factor, BLK, features)
            .sum(axis=2)
        )
        paired = segment.reshape(2, group_count // 2, 2, BLK, features)
        restored = jnp.concatenate([paired[:, :, 1:], paired[:, :, :1]], axis=2).reshape(
            2, group_count * BLK, features
        )
        level_grads.append(restored)
    sibling_grads = []
    for level_idx in range(cross_levels):
        sibling_grads.append(far_grads[:, level_idx * BLK : (level_idx + 1) * BLK])
    carried = jnp.zeros((2, BLK, features), jnp.float32)
    for level_idx in reversed(range(cross_levels)):
        outgoing = sibling_grads[level_idx]
        if level_idx + 1 < cross_levels:
            halves = spread_rows(carried, 2)
            lower_part = halves[:, :BLK]
            upper_part = halves[:, BLK:]
            upper_half = jnp.right_shift(where_seq, level_idx) & 1 == 1
            own_part = jnp.where(upper_half, upper_part, lower_part)
            outgoing = outgoing + jnp.where(upper_half, lower_part, upper_part)
        else:
            own_part = jnp.zeros_like(outgoing)
        carried = own_part + swapped(outgoing, "seq", level_idx)
    attended_blocks, carried = lax.optimization_barrier((attended_blocks, carried))
    output_sum = jnp.dot(attended_blocks[0], weight_cols[0], preferred_element_type=jnp.float32)
    for dist in range(1, len(attended_blocks)):
        output_sum = output_sum + jnp.dot(
            attended_blocks[dist], weight_cols[dist], preferred_element_type=jnp.float32
        )
    output = output_sum.astype(jnp.bfloat16)
    if local_levels:
        pooled_grad = level_grads[-1]
        for level_idx in reversed(range(local_levels - 1)):
            pooled_grad = level_grads[level_idx] + spread_rows(pooled_grad, 2)
        token_grad = token_grad + pooled_grad
    token_grad = token_grad + spread_rows(carried, 2**local_levels)
    grad_keys = token_grad[0].astype(jnp.bfloat16)
    grad_values = token_grad[1].astype(jnp.bfloat16)
    return (output, grad_query, grad_keys, grad_values, grad_weight)


def solution(mesh):
    placed = (
        P("seq", "head"),
        P("seq", "head"),
        P("seq", "head"),
        P("head", None),
        P("seq", "head"),
        P("seq", None),
    )
    return jax.shard_map(
        body,
        mesh=mesh,
        in_specs=placed,
        out_specs=(
            P("seq", "head"),
            P("seq", "head"),
            P("seq", "head"),
            P("seq", "head"),
            P("seq", "head"),
        ),
        check_vma=False,
    )
```
